256 devices in a mesh: seq: 8 (over z_hi, core), chan: 16 (over y, x), dp: 2 (over z_lo).
Axes of the slice: x: 4, y: 4, z: 8 (z_hi: 4, z_lo: 2; z = z_hi * 2 + z_lo), core: 2. Of those that a mesh axis runs over, the one named last changes fastest.
Arguments:
- query_proj: bfloat16 [2, 4096, 8192], P('dp', 'seq', 'chan'), may hold values from -6 to 6
- key_proj: bfloat16 [2, 4096, 8192], P('dp', 'seq', 'chan')
- value_proj: bfloat16 [2, 4096, 8192], P('dp', 'seq', 'chan')
- cotangent: bfloat16 [2, 4096, 8192], P('dp', 'seq', 'chan'), may hold values from -6 to 6
- long_filter: float32 [4096, 8192], P('seq', 'chan')
- skip_gain: float32 [8192], P('chan'), may hold values from -3 to 3
Outputs:
- output: bfloat16 [2, 4096, 8192], P('dp', 'seq', 'chan')
- grad_query: bfloat16 [2, 4096, 8192], P('dp', 'seq', 'chan')
- grad_key: bfloat16 [2, 4096, 8192], P('dp', 'seq', 'chan')
- grad_value: bfloat16 [2, 4096, 8192], P('dp', 'seq', 'chan')
- grad_filter: float32 [4096, 8192], P('seq', 'chan')
- grad_skip: float32 [8192], P('chan')
The draws below stay inside these ranges and needn't reach their ends.
All inputs are finite; a program needn't handle non-finite values.
Results may differ from the reference program's by a relative error of at most 0.0095.
Values may be sent and summed in bfloat16 or wider, within the bound.
No kernel may reach another device: no remote copies, remote signals or barrier semaphores. Data moves between devices by JAX's collectives and lax.ppermute only.
A program may use at most 64 MiB of HBM per device.

```python
import math
import jax
import jax.numpy as jnp
from jax import lax

D = 8192
L = 4096
B = 2


def draw_long_filter(key, part):
    unit = jax.random.uniform(jax.random.fold_in(key, 11), (D,), jnp.float32)
    lowest = math.log(0.5 / L)
    highest = math.log(1.0 / 32.0)
    positions = jnp.arange(L).astype(jnp.float32)
    rate = jnp.exp(lowest + unit * (highest - lowest))
    noise = jax.random.normal(jax.random.fold_in(key, 13), (L, D), jnp.float32)
    envelope = jnp.sqrt(2.0 * rate)[None, :] * jnp.exp(-rate[None, :] * positions[:, None])
    tail_height = jax.random.uniform(jax.random.fold_in(key, 14), (D,), jnp.float32, 0.8, 1.2) * (0.0077 / math.sqrt(L))
    tail = tail_height[None, :] * jnp.exp(-positions[:, None] / float(L))
    return (noise * envelope + tail).astype(jnp.float32)


def shared_offset(key):
    base = jax.random.fold_in(key, 21)
    amplitude = jax.random.uniform(jax.random.fold_in(base, 1), (B, 1, D), jnp.float32, 0.6, 1.2)
    flip = jax.random.uniform(jax.random.fold_in(base, 2), (B, 1, D), jnp.float32)
    sign_part = jnp.where(flip < 0.5, -1.0, 1.0).astype(jnp.float32)
    phase = jax.random.uniform(jax.random.fold_in(base, 3), (B, 1, D), jnp.float32, -math.pi, math.pi)
    positions = jnp.arange(L).astype(jnp.float32)[None, :, None]
    return sign_part * amplitude * (0.8 + 0.4 * jnp.cos(2.0 * math.pi / L * positions + phase))


def branch_noise(key, salt):
    noise = jnp.clip(jax.random.normal(jax.random.fold_in(key, salt), (B, L, D), jnp.float32), -4.0, 4.0)
    return noise


def draw_key_proj(key, part):
    values = shared_offset(key) + branch_noise(key, 22)
    return jnp.clip(values, -6.0, 6.0).astype(jnp.bfloat16)


def draw_value_proj(key, part):
    values = shared_offset(key) + branch_noise(key, 23)
    return jnp.clip(values, -6.0, 6.0).astype(jnp.bfloat16)


def block_scale(stream_key, dims, shards, least, top_value):
    loudness = 1.0
    for dim, blocks in shards:
        steps = jax.random.uniform(jax.random.fold_in(jax.random.fold_in(stream_key, 6), dim), (blocks,), jnp.float32, least / len(shards), top_value / len(shards))
        loudness = loudness * jnp.repeat(jnp.exp(steps), dims[dim] // blocks).reshape((-1,) + (1,) * (len(dims) - 1 - dim))
    return loudness


def centred(own_key, dims, scale, reach, split=(), kind=jnp.bfloat16):
    entries = jax.random.normal(own_key, dims, jnp.float32) * scale
    if len(split) > 0:
        entries = block_scale(own_key, dims, split, -0.22, 0.18) * entries
    return jnp.clip(entries, min=-reach, max=reach).astype(kind)


def setup_inputs(seed: int = 0) -> dict:
    key_list = jax.random.split(jax.random.key(seed), 7)
    return {
        "query_proj": centred(key_list[0], (B, L, D), 1.0, 6.0, ((0, 2), (1, 8), (2, 16))),
        "key_proj": draw_key_proj(jax.random.fold_in(key_list[6], 71), 0),
        "value_proj": draw_value_proj(jax.random.fold_in(key_list[6], 71), 0),
        "cotangent": centred(key_list[3], (B, L, D), 1.0, 6.0, ((0, 2), (1, 8), (2, 16))),
        "long_filter": draw_long_filter(jax.random.fold_in(key_list[6], 71), 0),
        "skip_gain": centred(key_list[5], (D,), 0.5, 3.0, ((0, 16),), jnp.float32),
    }


def channel_block(items):
    query_blk, key_blk, value_blk, cot_blk, filter_blk, skip_blk = items
    full_size = 2 * L
    kernel = filter_blk.astype(jnp.float32)
    mixed = (key_blk.astype(jnp.float32) * value_blk.astype(jnp.float32)).astype(jnp.bfloat16)
    weighted = (cot_blk.astype(jnp.float32) * query_blk.astype(jnp.float32)).astype(jnp.bfloat16)
    mixed_wide = mixed.astype(jnp.float32)
    weighted_wide = weighted.astype(jnp.float32)
    mixed_spec = jnp.fft.rfft(mixed_wide, n=full_size, axis=1)
    weighted_spec = jnp.fft.rfft(weighted_wide, n=full_size, axis=1)
    kernel_spec = jnp.fft.rfft(kernel, n=full_size, axis=0)[None]
    conv_vals = jnp.fft.irfft(mixed_spec * kernel_spec, n=full_size, axis=1)[:, :L].astype(jnp.bfloat16)
    corr_vals = jnp.fft.irfft(jnp.conj(kernel_spec) * weighted_spec, n=full_size, axis=1)[:, :L].astype(jnp.bfloat16)
    signal = conv_vals.astype(jnp.float32) + skip_blk[None, None, :] * mixed_wide
    output = (query_blk.astype(jnp.float32) * signal).astype(jnp.bfloat16)
    grad_query = (cot_blk.astype(jnp.float32) * signal).astype(jnp.bfloat16)
    back = corr_vals.astype(jnp.float32) + skip_blk[None, None, :] * weighted_wide
    grad_key = (back * value_blk.astype(jnp.float32)).astype(jnp.bfloat16)
    grad_value = (back * key_blk.astype(jnp.float32)).astype(jnp.bfloat16)
    slope_spec = jnp.sum(jnp.conj(mixed_spec) * weighted_spec, axis=0)
    slope = jnp.fft.irfft(slope_spec, n=full_size, axis=0)[:L]
    factor = (B * L) ** -0.5
    grad_filt = factor * slope
    grad_gain = factor * jnp.sum(weighted_wide * mixed_wide, axis=(0, 1))
    return output, grad_query, grad_key, grad_value, grad_filt, grad_gain


def reference(query_proj, key_proj, value_proj, cotangent, long_filter, skip_gain):
    block_width = min(D, 512)
    block_count = D // block_width

    def stack_blocks(arr):
        return jnp.moveaxis(arr.reshape(B, L, block_count, block_width), 2, 0)

    items = (stack_blocks(query_proj), stack_blocks(key_proj), stack_blocks(value_proj), stack_blocks(cotangent),
             jnp.moveaxis(long_filter.reshape(L, block_count, block_width), 1, 0),
             skip_gain.reshape(block_count, block_width))
    results = lax.map(channel_block, items)

    def unstack_blocks(arr):
        return jnp.moveaxis(arr, 0, 2).reshape(B, L, D)

    output, grad_query, grad_key, grad_value, grad_filt, grad_gain = results
    return (unstack_blocks(output), unstack_blocks(grad_query), unstack_blocks(grad_key), unstack_blocks(grad_value),
            jnp.moveaxis(grad_filt, 0, 1).reshape(L, D), grad_gain.reshape(D))
```

```python
import math

import jax
import jax.numpy as jnp
from jax import lax
from jax.sharding import PartitionSpec as P

full_precision = lax.Precision.HIGHEST


def spectral_tables(seq_length):
    full_size = 2 * seq_length
    inner = 128
    outer = full_size // inner
    rows = seq_length // inner
    half = outer // 2 + 1
    k_index = jnp.arange(half, dtype=jnp.int32)
    n_index = jnp.arange(rows, dtype=jnp.int32)
    m_index = jnp.arange(inner, dtype=jnp.int32)
    j_index = jnp.arange(inner, dtype=jnp.int32)
    first_angle = (2.0 * math.pi / outer) * (
        (k_index[:, None] * n_index[None, :]) % outer
    ).astype(jnp.float32)
    first_cos = jnp.cos(first_angle)
    first_sin = jnp.sin(first_angle)
    stage_a = jnp.concatenate([first_cos, -first_sin], axis=0)
    weight = jnp.where((k_index == 0) | (k_index == outer // 2), 1.0, 2.0) / full_size
    inv_a = jnp.concatenate(
        [(first_cos * weight[:, None]).T, (-first_sin * weight[:, None]).T], axis=1
    )
    twist_angle = (2.0 * math.pi / full_size) * (
        (k_index[:, None] * m_index[None, :]) % full_size
    ).astype(jnp.float32)
    twist_cos, twist_sin = jnp.cos(twist_angle), jnp.sin(twist_angle)
    last_angle = (2.0 * math.pi / inner) * (
        (j_index[:, None] * m_index[None, :]) % inner
    ).astype(jnp.float32)
    last_cos, last_sin = jnp.cos(last_angle), jnp.sin(last_angle)
    g_re = twist_cos[:, None, :] * last_cos[None] - twist_sin[:, None, :] * last_sin[None]
    g_im = -(twist_sin[:, None, :] * last_cos[None] + twist_cos[:, None, :] * last_sin[None])
    fwd_table = jnp.concatenate([g_re, g_im], axis=1).astype(jnp.bfloat16)
    g_re_t = jnp.swapaxes(g_re, 1, 2)
    g_im_t = jnp.swapaxes(g_im, 1, 2)
    inv_table = jnp.concatenate([g_re_t, -g_im_t], axis=1).astype(jnp.bfloat16)
    return stage_a, inv_a, fwd_table, inv_table


def complex_stage(table, real_part, imag_part):
    inner = real_part.shape[1]
    a = jnp.einsum(
        "kjm,kml->kjl", table, real_part.astype(jnp.bfloat16),
        preferred_element_type=jnp.float32,
    )
    b = jnp.einsum(
        "kjm,kml->kjl", table, imag_part.astype(jnp.bfloat16),
        preferred_element_type=jnp.float32,
    )
    out_real = a[:, :inner] - b[:, inner:]
    out_imag = b[:, :inner] + a[:, inner:]
    return out_real, out_imag


def spectral_block(signals, taps):
    seq_length, _, batches, width = signals.shape
    stage_a, inv_a, fwd_table, inv_table = spectral_tables(seq_length)
    inner = fwd_table.shape[2]
    rows = seq_length // inner
    half = fwd_table.shape[0]
    lanes = 2 * batches * width + width
    stacked = jnp.concatenate(
        [signals.reshape(seq_length, 2 * batches * width), taps], axis=1
    ).reshape(rows, inner * lanes)
    first = jnp.dot(stage_a, stacked, precision=full_precision).reshape(
        2, half, inner, lanes
    )
    spec_re, spec_im = complex_stage(fwd_table, first[0], first[1])
    sig_count = batches * width
    mixed_re = spec_re[..., :sig_count].reshape(half, inner, batches, width)
    mixed_im = spec_im[..., :sig_count].reshape(half, inner, batches, width)
    weighted_re = spec_re[..., sig_count : 2 * sig_count].reshape(half, inner, batches, width)
    weighted_im = spec_im[..., sig_count : 2 * sig_count].reshape(half, inner, batches, width)
    taps_re = spec_re[..., 2 * sig_count :][:, :, None, :]
    taps_im = spec_im[..., 2 * sig_count :][:, :, None, :]
    conv_re = mixed_re * taps_re - mixed_im * taps_im
    conv_im = mixed_re * taps_im + mixed_im * taps_re
    corr_re = taps_re * weighted_re + taps_im * weighted_im
    corr_im = taps_re * weighted_im - taps_im * weighted_re
    slope_re = jnp.sum(mixed_re * weighted_re + mixed_im * weighted_im, axis=2)
    slope_im = jnp.sum(mixed_re * weighted_im - mixed_im * weighted_re, axis=2)
    prod_re = jnp.concatenate(
        [conv_re.reshape(half, inner, sig_count), corr_re.reshape(half, inner, sig_count), slope_re],
        axis=2,
    )
    prod_im = jnp.concatenate(
        [conv_im.reshape(half, inner, sig_count), corr_im.reshape(half, inner, sig_count), slope_im],
        axis=2,
    )
    back_re, back_im = complex_stage(inv_table, prod_re, prod_im)
    both = jnp.concatenate([back_re, back_im], axis=0).reshape(2 * half, inner * lanes)
    result = jnp.dot(inv_a, both, precision=full_precision).reshape(seq_length, lanes)
    pair = result[:, : 2 * sig_count].reshape(seq_length, 2, batches, width)
    slope = result[:, 2 * sig_count :]
    return pair, slope


def on_device(query_proj, key_proj, value_proj, cotangent, long_filter, skip_gain):
    query_rows = query_proj[0].astype(jnp.float32)
    key_rows = key_proj[0].astype(jnp.float32)
    value_rows = value_proj[0].astype(jnp.float32)
    cot_rows = cotangent[0].astype(jnp.float32)
    local_length, chan_width = query_proj.shape[1], query_proj.shape[2]
    seq_count = lax.axis_size("seq")
    batch_count = lax.axis_size("dp")
    groups = seq_count * batch_count
    share = chan_width // groups
    seq_length = seq_count * local_length
    factor = (batch_count * seq_length) ** (-0.5)
    mixed = (key_rows * value_rows).astype(jnp.bfloat16)
    weighted = (cot_rows * query_rows).astype(jnp.bfloat16)

    pair = jnp.stack([mixed.T, weighted.T], axis=0).reshape(2, groups, share, local_length)
    pair = jnp.transpose(pair, (1, 0, 2, 3))
    pair_cols = lax.all_to_all(pair, ("seq", "dp"), 0, 0, tiled=True)
    taps_t = long_filter.T.reshape(seq_count, batch_count, share, local_length)
    taps_mine = lax.dynamic_index_in_dim(taps_t, lax.axis_index("dp"), axis=1, keepdims=False)
    taps_cols = lax.all_to_all(taps_mine, "seq", 0, 0, tiled=True)

    pair_f = pair_cols.reshape(seq_count, batch_count, 2, share, local_length).astype(jnp.float32)
    grad_skip_part = factor * jnp.sum(pair_f[:, :, 0] * pair_f[:, :, 1], axis=(0, 1, 3))
    grad_skip = lax.all_gather(grad_skip_part, ("seq", "dp"), axis=0, tiled=True)
    signals = jnp.transpose(pair_f, (0, 4, 2, 1, 3)).reshape(seq_length, 2, batch_count, share)
    taps = jnp.transpose(taps_cols, (0, 2, 1)).reshape(seq_length, share)

    pair_vals, slope = spectral_block(signals, taps)

    pair_back = pair_vals.astype(jnp.bfloat16).reshape(
        seq_count, local_length, 2, batch_count, share
    )
    pair_back = jnp.transpose(pair_back, (0, 3, 2, 1, 4))
    pair_back = jnp.swapaxes(pair_back, 3, 4).reshape(groups, 2, share, local_length)
    pair_home = lax.all_to_all(pair_back, ("seq", "dp"), 0, 0, tiled=True)
    pair_home = jnp.transpose(pair_home, (1, 0, 2, 3)).reshape(2, chan_width, local_length)
    conv_rows = pair_home[0].T.astype(jnp.float32)
    corr_rows = pair_home[1].T.astype(jnp.float32)

    slope_blocks = jnp.swapaxes(slope.reshape(seq_count, local_length, share), 1, 2)
    slope_send = jnp.broadcast_to(
        slope_blocks[:, None], (seq_count, batch_count, share, local_length)
    ).reshape(groups, share, local_length)
    slope_home = lax.all_to_all(slope_send, ("seq", "dp"), 0, 0, tiled=True)
    grad_filter = factor * slope_home.reshape(chan_width, local_length).T

    mixed_wide = mixed.astype(jnp.float32)
    weighted_wide = weighted.astype(jnp.float32)
    signal = conv_rows + skip_gain[None, :] * mixed_wide
    output = (query_rows * signal).astype(jnp.bfloat16)
    grad_query = (cot_rows * signal).astype(jnp.bfloat16)
    back = corr_rows + skip_gain[None, :] * weighted_wide
    grad_key = (back * value_rows).astype(jnp.bfloat16)
    grad_value = (back * key_rows).astype(jnp.bfloat16)
    return (
        output[None],
        grad_query[None],
        grad_key[None],
        grad_value[None],
        grad_filter,
        grad_skip,
    )


def solution(mesh):
    return jax.shard_map(
        on_device,
        mesh=mesh,
        in_specs=(
            P("dp", "seq", "chan"),
            P("dp", "seq", "chan"),
            P("dp", "seq", "chan"),
            P("dp", "seq", "chan"),
            P("seq", "chan"),
            P("chan"),
        ),
        out_specs=(
            P("dp", "seq", "chan"),
            P("dp", "seq", "chan"),
            P("dp", "seq", "chan"),
            P("dp", "seq", "chan"),
            P("seq", "chan"),
            P("chan"),
        ),
        check_vma=False,
    )
```

```python
import math

import jax
import jax.numpy as jnp
from jax import lax
from jax.sharding import PartitionSpec as P

full_precision = lax.Precision.HIGHEST


def spectral_tables(seq_length):
    full_size = 2 * seq_length
    inner = 128
    outer = full_size // inner
    rows = seq_length // inner
    half = outer // 2 + 1
    k_index = jnp.arange(half, dtype=jnp.int32)
    n_index = jnp.arange(rows, dtype=jnp.int32)
    m_index = jnp.arange(inner, dtype=jnp.int32)
    j_index = jnp.arange(inner, dtype=jnp.int32)
    first_angle = (2.0 * math.pi / outer) * (
        (k_index[:, None] * n_index[None, :]) % outer
    ).astype(jnp.float32)
    first_cos = jnp.cos(first_angle)
    first_sin = jnp.sin(first_angle)
    stage_a = jnp.concatenate([first_cos, -first_sin], axis=0)
    weight = jnp.where((k_index == 0) | (k_index == outer // 2), 1.0, 2.0) / full_size
    inv_a = jnp.concatenate(
        [(first_cos * weight[:, None]).T, (-first_sin * weight[:, None]).T], axis=1
    )
    twist_angle = (2.0 * math.pi / full_size) * (
        (k_index[:, None] * m_index[None, :]) % full_size
    ).astype(jnp.float32)
    twist_cos, twist_sin = jnp.cos(twist_angle), jnp.sin(twist_angle)
    last_angle = (2.0 * math.pi / inner) * (
        (j_index[:, None] * m_index[None, :]) % inner
    ).astype(jnp.float32)
    last_cos, last_sin = jnp.cos(last_angle), jnp.sin(last_angle)
    g_re = twist_cos[:, None, :] * last_cos[None] - twist_sin[:, None, :] * last_sin[None]
    g_im = -(twist_sin[:, None, :] * last_cos[None] + twist_cos[:, None, :] * last_sin[None])
    fwd_table = jnp.concatenate([g_re, g_im], axis=1).astype(jnp.bfloat16)
    g_re_t = jnp.swapaxes(g_re, 1, 2)
    g_im_t = jnp.swapaxes(g_im, 1, 2)
    inv_table = jnp.concatenate([g_re_t, -g_im_t], axis=1).astype(jnp.bfloat16)
    return stage_a, inv_a, fwd_table, inv_table


def complex_stage(table, real_part, imag_part):
    inner = real_part.shape[1]
    a = jnp.einsum(
        "kjm,kml->kjl", table, real_part.astype(jnp.bfloat16),
        preferred_element_type=jnp.float32,
    )
    b = jnp.einsum(
        "kjm,kml->kjl", table, imag_part.astype(jnp.bfloat16),
        preferred_element_type=jnp.float32,
    )
    out_real = a[:, :inner] - b[:, inner:]
    out_imag = b[:, :inner] + a[:, inner:]
    return out_real, out_imag


def forward_spectrum(slab, tables):
    stage_a, _, fwd_table, _ = tables
    half = fwd_table.shape[0]
    first = jnp.einsum("kn,nml->kml", stage_a, slab, precision=full_precision)
    return complex_stage(fwd_table, first[:half], first[half:])


def inverse_spectrum(prod_re, prod_im, tables):
    _, inv_a, _, inv_table = tables
    back_re, back_im = complex_stage(inv_table, prod_re, prod_im)
    both = jnp.concatenate([back_re, back_im], axis=0)
    return jnp.einsum("nk,kml->nml", inv_a, both, precision=full_precision)


def spectral_block(signals, taps):
    seq_length, lanes = signals.shape
    tables = spectral_tables(seq_length)
    inner = tables[2].shape[2]
    rows = seq_length // inner
    half_lanes = lanes // 2
    sig_re, sig_im = forward_spectrum(signals.reshape(rows, inner, lanes), tables)
    taps_re, taps_im = forward_spectrum(taps.reshape(rows, inner, lanes), tables)
    lane = lax.broadcasted_iota(jnp.int32, (1, 1, lanes), 2)
    taps_im = jnp.where(lane < half_lanes, taps_im, -taps_im)
    pair_re = sig_re * taps_re - sig_im * taps_im
    pair_im = sig_re * taps_im + sig_im * taps_re
    turned_re = jnp.roll(sig_re, half_lanes, axis=2)
    turned_im = jnp.roll(sig_im, half_lanes, axis=2)
    cross_re = sig_re * turned_re + sig_im * turned_im
    cross_im = sig_re * turned_im - sig_im * turned_re
    pair = inverse_spectrum(pair_re, pair_im, tables).reshape(seq_length, lanes)
    cross = inverse_spectrum(cross_re, cross_im, tables).reshape(seq_length, lanes)
    return pair, cross


def on_device(query_proj, key_proj, value_proj, cotangent, long_filter, skip_gain):
    query_rows = query_proj[0].astype(jnp.float32)
    key_rows = key_proj[0].astype(jnp.float32)
    value_rows = value_proj[0].astype(jnp.float32)
    cot_rows = cotangent[0].astype(jnp.float32)
    local_length, chan_width = query_proj.shape[1], query_proj.shape[2]
    seq_count = lax.axis_size("seq")
    batch_count = lax.axis_size("dp")
    groups = seq_count * batch_count
    share = chan_width // groups
    seq_length = seq_count * local_length
    factor = (batch_count * seq_length) ** (-0.5)
    mixed = (key_rows * value_rows).astype(jnp.bfloat16)
    weighted = (cot_rows * query_rows).astype(jnp.bfloat16)

    pair = jnp.stack([mixed.T, weighted.T], axis=0).reshape(2, groups, share, local_length)
    pair = jnp.transpose(pair, (1, 0, 2, 3))
    pair_cols = lax.all_to_all(pair, ("seq", "dp"), 0, 0, tiled=True)
    taps_t = long_filter.T.reshape(seq_count, batch_count, share, local_length)
    taps_mine = lax.dynamic_index_in_dim(taps_t, lax.axis_index("dp"), axis=1, keepdims=False)
    taps_cols = lax.all_to_all(taps_mine, "seq", 0, 0, tiled=True)

    mixed_wide = mixed.astype(jnp.float32)
    weighted_wide = weighted.astype(jnp.float32)
    gain_part = jnp.sum(weighted_wide * mixed_wide, axis=0)
    grad_skip = factor * lax.psum(gain_part, ("seq", "dp"))
    grad_skip, pair_cols, taps_cols = lax.optimization_barrier((grad_skip, pair_cols, taps_cols))

    pair_t = pair_cols.reshape(seq_count, batch_count, 2, share, local_length)
    signals = jnp.transpose(pair_t, (0, 4, 2, 1, 3)).reshape(seq_length, 2 * batch_count * share)
    taps = jnp.transpose(taps_cols, (0, 2, 1)).reshape(seq_length, 1, share)
    taps = jnp.broadcast_to(taps, (seq_length, 2 * batch_count, share)).reshape(
        seq_length, 2 * batch_count * share
    )

    pair_vals, cross = spectral_block(signals.astype(jnp.float32), taps)
    pair_vals = pair_vals.reshape(seq_length, 2, batch_count, share)
    cross = cross.reshape(seq_length, 2, batch_count, share)
    slope = jnp.sum(cross[:, 0], axis=1)

    pair_back = pair_vals.astype(jnp.bfloat16).reshape(
        seq_count, local_length, 2, batch_count, share
    )
    pair_back = jnp.transpose(pair_back, (0, 3, 2, 1, 4))
    pair_back = jnp.swapaxes(pair_back, 3, 4).reshape(groups, 2, share, local_length)
    pair_home = lax.all_to_all(pair_back, ("seq", "dp"), 0, 0, tiled=True)
    pair_home = jnp.transpose(pair_home, (1, 0, 2, 3)).reshape(2, chan_width, local_length)
    conv_rows = pair_home[0].T.astype(jnp.float32)
    corr_rows = pair_home[1].T.astype(jnp.float32)

    slope_blocks = jnp.swapaxes(slope.reshape(seq_count, local_length, share), 1, 2)
    slope_send = jnp.broadcast_to(
        slope_blocks[:, None], (seq_count, batch_count, share, local_length)
    ).reshape(groups, share, local_length)
    slope_home = lax.all_to_all(slope_send, ("seq", "dp"), 0, 0, tiled=True)
    grad_filter = factor * slope_home.reshape(chan_width, local_length).T

    signal = conv_rows + skip_gain[None, :] * mixed_wide
    output = (query_rows * signal).astype(jnp.bfloat16)
    grad_query = (cot_rows * signal).astype(jnp.bfloat16)
    back = corr_rows + skip_gain[None, :] * weighted_wide
    grad_key = (back * value_rows).astype(jnp.bfloat16)
    grad_value = (back * key_rows).astype(jnp.bfloat16)
    return (
        output[None],
        grad_query[None],
        grad_key[None],
        grad_value[None],
        grad_filter,
        grad_skip,
    )


def solution(mesh):
    return jax.shard_map(
        on_device,
        mesh=mesh,
        in_specs=(
            P("dp", "seq", "chan"),
            P("dp", "seq", "chan"),
            P("dp", "seq", "chan"),
            P("dp", "seq", "chan"),
            P("seq", "chan"),
            P("chan"),
        ),
        out_specs=(
            P("dp", "seq", "chan"),
            P("dp", "seq", "chan"),
            P("dp", "seq", "chan"),
            P("dp", "seq", "chan"),
            P("seq", "chan"),
            P("chan"),
        ),
        check_vma=False,
    )
```

```python
import math

import jax
import jax.numpy as jnp
from jax import lax
from jax.sharding import PartitionSpec as P

full_precision = lax.Precision.HIGHEST


def spectral_tables(seq_length):
    full_size = 2 * seq_length
    inner = 128
    outer = full_size // inner
    rows = seq_length // inner
    half = outer // 2 + 1
    k_index = jnp.arange(half, dtype=jnp.int32)
    n_index = jnp.arange(rows, dtype=jnp.int32)
    m_index = jnp.arange(inner, dtype=jnp.int32)
    j_index = jnp.arange(inner, dtype=jnp.int32)
    first_angle = (2.0 * math.pi / outer) * (
        (k_index[:, None] * n_index[None, :]) % outer
    ).astype(jnp.float32)
    first_cos = jnp.cos(first_angle)
    first_sin = jnp.sin(first_angle)
    stage_a = jnp.concatenate([first_cos, -first_sin], axis=0)
    weight = jnp.where((k_index == 0) | (k_index == outer // 2), 1.0, 2.0) / full_size
    inv_a = jnp.concatenate(
        [(first_cos * weight[:, None]).T, (-first_sin * weight[:, None]).T], axis=1
    )
    twist_angle = (2.0 * math.pi / full_size) * (
        (k_index[:, None] * m_index[None, :]) % full_size
    ).astype(jnp.float32)
    twist_cos, twist_sin = jnp.cos(twist_angle), jnp.sin(twist_angle)
    last_angle = (2.0 * math.pi / inner) * (
        (j_index[:, None] * m_index[None, :]) % inner
    ).astype(jnp.float32)
    last_cos, last_sin = jnp.cos(last_angle), jnp.sin(last_angle)
    g_re = twist_cos[:, None, :] * last_cos[None] - twist_sin[:, None, :] * last_sin[None]
    g_im = -(twist_sin[:, None, :] * last_cos[None] + twist_cos[:, None, :] * last_sin[None])
    fwd_table = jnp.concatenate([g_re, g_im], axis=1).astype(jnp.bfloat16)
    g_re_t = jnp.swapaxes(g_re, 1, 2)
    g_im_t = jnp.swapaxes(g_im, 1, 2)
    inv_table = jnp.concatenate([g_re_t, -g_im_t], axis=1).astype(jnp.bfloat16)
    return stage_a, inv_a, fwd_table, inv_table


def complex_stage(table, real_part, imag_part):
    inner = real_part.shape[1]
    a = jnp.einsum(
        "kjm,kml->kjl", table, real_part.astype(jnp.bfloat16),
        preferred_element_type=jnp.float32,
    )
    b = jnp.einsum(
        "kjm,kml->kjl", table, imag_part.astype(jnp.bfloat16),
        preferred_element_type=jnp.float32,
    )
    out_real = a[:, :inner] - b[:, inner:]
    out_imag = b[:, :inner] + a[:, inner:]
    return out_real, out_imag


def forward_spectrum(slab, tables):
    stage_a, _, fwd_table, _ = tables
    half = fwd_table.shape[0]
    first = jnp.einsum("kn,nml->kml", stage_a, slab, precision=full_precision)
    return complex_stage(fwd_table, first[:half], first[half:])


def inverse_spectrum(prod_re, prod_im, tables):
    _, inv_a, _, inv_table = tables
    back_re, back_im = complex_stage(inv_table, prod_re, prod_im)
    both = jnp.concatenate([back_re, back_im], axis=0)
    return jnp.einsum("nk,kml->nml", inv_a, both, precision=full_precision)


def spectral_block(signals, taps):
    seq_length, lanes = signals.shape
    tables = spectral_tables(seq_length)
    inner = tables[2].shape[2]
    rows = seq_length // inner
    half_lanes = lanes // 2
    sig_re, sig_im = forward_spectrum(signals.reshape(rows, inner, lanes), tables)
    taps_re, taps_im = forward_spectrum(taps.reshape(rows, inner, lanes), tables)
    lane = lax.broadcasted_iota(jnp.int32, (1, 1, lanes), 2)
    taps_im = jnp.where(lane < half_lanes, taps_im, -taps_im)
    pair_re = sig_re * taps_re - sig_im * taps_im
    pair_im = sig_re * taps_im + sig_im * taps_re
    turned_re = jnp.roll(sig_re, half_lanes, axis=2)
    turned_im = jnp.roll(sig_im, half_lanes, axis=2)
    cross_re = sig_re * turned_re + sig_im * turned_im
    cross_im = sig_re * turned_im - sig_im * turned_re
    pair = inverse_spectrum(pair_re, pair_im, tables).reshape(seq_length, lanes)
    cross = inverse_spectrum(cross_re, cross_im, tables).reshape(seq_length, lanes)
    return pair, cross


def on_device(query_proj, key_proj, value_proj, cotangent, long_filter, skip_gain):
    query_rows = query_proj[0].astype(jnp.float32)
    key_rows = key_proj[0].astype(jnp.float32)
    value_rows = value_proj[0].astype(jnp.float32)
    cot_rows = cotangent[0].astype(jnp.float32)
    local_length, chan_width = query_proj.shape[1], query_proj.shape[2]
    seq_count = lax.axis_size("seq")
    batch_count = lax.axis_size("dp")
    groups = seq_count * batch_count
    share = chan_width // groups
    seq_length = seq_count * local_length
    factor = (batch_count * seq_length) ** (-0.5)
    mixed = (key_rows * value_rows).astype(jnp.bfloat16)
    weighted = (cot_rows * query_rows).astype(jnp.bfloat16)

    mixed_wide = mixed.astype(jnp.float32)
    weighted_wide = weighted.astype(jnp.float32)
    gain_part = jnp.sum(weighted_wide * mixed_wide, axis=0)
    grad_skip = factor * lax.psum(gain_part, ("seq", "dp"))

    pair = jnp.stack([mixed.T, weighted.T], axis=0).reshape(2, groups, share, local_length)
    pair = jnp.transpose(pair, (1, 0, 2, 3)).reshape(groups, 2 * share, local_length)
    half_length = local_length // batch_count
    taps_t = long_filter.T.reshape(groups, share, batch_count, half_length)
    taps_mine = lax.dynamic_index_in_dim(taps_t, lax.axis_index("dp"), axis=2, keepdims=False)
    taps_rows = share * half_length // local_length
    taps_mine = taps_mine.astype(jnp.bfloat16).reshape(groups, taps_rows, local_length)
    send = jnp.concatenate([pair, taps_mine], axis=1)
    grad_skip, send = lax.optimization_barrier((grad_skip, send))
    got = lax.all_to_all(send, ("seq", "dp"), 0, 0, tiled=True)

    pair_t = got[:, : 2 * share].reshape(seq_count, batch_count, 2, share, local_length)
    signals = jnp.transpose(pair_t, (0, 4, 2, 1, 3)).reshape(seq_length, 2 * batch_count * share)
    taps_t = got[:, 2 * share :].reshape(seq_count, batch_count, share, half_length)
    taps = jnp.transpose(taps_t, (0, 1, 3, 2)).reshape(seq_length, 1, share)
    taps = jnp.broadcast_to(taps, (seq_length, 2 * batch_count, share)).reshape(
        seq_length, 2 * batch_count * share
    )

    pair_vals, cross = spectral_block(signals.astype(jnp.float32), taps.astype(jnp.float32))
    pair_vals = pair_vals.reshape(seq_length, 2, batch_count, share)
    cross = cross.reshape(seq_length, 2, batch_count, share)
    slope = jnp.sum(cross[:, 0], axis=1)

    pair_back = pair_vals.astype(jnp.bfloat16).reshape(
        seq_count, local_length, 2, batch_count, share
    )
    pair_back = jnp.transpose(pair_back, (0, 3, 2, 4, 1)).reshape(
        groups, 2 * share, local_length
    )
    slope_blocks = jnp.swapaxes(slope.astype(jnp.bfloat16).reshape(seq_count, local_length, share), 1, 2)
    slope_send = jnp.broadcast_to(
        slope_blocks[:, None], (seq_count, batch_count, share, local_length)
    ).reshape(groups, share, local_length)
    home = lax.all_to_all(
        jnp.concatenate([pair_back, slope_send], axis=1), ("seq", "dp"), 0, 0, tiled=True
    )
    pair_home = home[:, : 2 * share].reshape(groups, 2, share, local_length)
    pair_home = jnp.transpose(pair_home, (1, 0, 2, 3)).reshape(2, chan_width, local_length)
    conv_rows = pair_home[0].T.astype(jnp.float32)
    corr_rows = pair_home[1].T.astype(jnp.float32)
    slope_home = home[:, 2 * share :].reshape(chan_width, local_length)
    grad_filter = factor * slope_home.T.astype(jnp.float32)

    signal = conv_rows + skip_gain[None, :] * mixed_wide
    output = (query_rows * signal).astype(jnp.bfloat16)
    grad_query = (cot_rows * signal).astype(jnp.bfloat16)
    back = corr_rows + skip_gain[None, :] * weighted_wide
    grad_key = (back * value_rows).astype(jnp.bfloat16)
    grad_value = (back * key_rows).astype(jnp.bfloat16)
    return (
        output[None],
        grad_query[None],
        grad_key[None],
        grad_value[None],
        grad_filter,
        grad_skip,
    )


def solution(mesh):
    return jax.shard_map(
        on_device,
        mesh=mesh,
        in_specs=(
            P("dp", "seq", "chan"),
            P("dp", "seq", "chan"),
            P("dp", "seq", "chan"),
            P("dp", "seq", "chan"),
            P("seq", "chan"),
            P("chan"),
        ),
        out_specs=(
            P("dp", "seq", "chan"),
            P("dp", "seq", "chan"),
            P("dp", "seq", "chan"),
            P("dp", "seq", "chan"),
            P("seq", "chan"),
            P("chan"),
        ),
        check_vma=False,
    )
```

```python
import math

import jax
import jax.numpy as jnp
from jax import lax
from jax.sharding import PartitionSpec as P

full_precision = lax.Precision.HIGHEST


def spectral_tables(seq_length):
    full_size = 2 * seq_length
    inner = 128
    outer = full_size // inner
    rows = seq_length // inner
    half = outer // 2 + 1
    k_index = jnp.arange(half, dtype=jnp.int32)
    n_index = jnp.arange(rows, dtype=jnp.int32)
    m_index = jnp.arange(inner, dtype=jnp.int32)
    j_index = jnp.arange(inner, dtype=jnp.int32)
    first_angle = (2.0 * math.pi / outer) * (
        (k_index[:, None] * n_index[None, :]) % outer
    ).astype(jnp.float32)
    first_cos = jnp.cos(first_angle)
    first_sin = jnp.sin(first_angle)
    stage_a = jnp.concatenate([first_cos, -first_sin], axis=0)
    weight = jnp.where((k_index == 0) | (k_index == outer // 2), 1.0, 2.0) / full_size
    inv_a = jnp.concatenate(
        [(first_cos * weight[:, None]).T, (-first_sin * weight[:, None]).T], axis=1
    )
    twist_angle = (2.0 * math.pi / full_size) * (
        (k_index[:, None] * m_index[None, :]) % full_size
    ).astype(jnp.float32)
    twist_cos, twist_sin = jnp.cos(twist_angle), jnp.sin(twist_angle)
    last_angle = (2.0 * math.pi / inner) * (
        (j_index[:, None] * m_index[None, :]) % inner
    ).astype(jnp.float32)
    last_cos, last_sin = jnp.cos(last_angle), jnp.sin(last_angle)
    g_re = twist_cos[:, None, :] * last_cos[None] - twist_sin[:, None, :] * last_sin[None]
    g_im = -(twist_sin[:, None, :] * last_cos[None] + twist_cos[:, None, :] * last_sin[None])
    fwd_table = jnp.concatenate([g_re, g_im], axis=1).astype(jnp.bfloat16)
    g_re_t = jnp.swapaxes(g_re, 1, 2)
    g_im_t = jnp.swapaxes(g_im, 1, 2)
    inv_table = jnp.concatenate([g_re_t, -g_im_t], axis=1).astype(jnp.bfloat16)
    return stage_a, inv_a, fwd_table, inv_table


def complex_stage(table, real_part, imag_part):
    inner = real_part.shape[1]
    a = jnp.einsum(
        "kjm,kml->kjl", table, real_part.astype(jnp.bfloat16),
        preferred_element_type=jnp.float32,
    )
    b = jnp.einsum(
        "kjm,kml->kjl", table, imag_part.astype(jnp.bfloat16),
        preferred_element_type=jnp.float32,
    )
    out_real = a[:, :inner] - b[:, inner:]
    out_imag = b[:, :inner] + a[:, inner:]
    return out_real, out_imag


def forward_spectrum(slab, tables):
    stage_a, _, fwd_table, _ = tables
    half = fwd_table.shape[0]
    first = jnp.einsum("kn,nml->kml", stage_a, slab, precision=full_precision)
    return complex_stage(fwd_table, first[:half], first[half:])


def inverse_spectrum(prod_re, prod_im, tables):
    _, inv_a, _, inv_table = tables
    back_re, back_im = complex_stage(inv_table, prod_re, prod_im)
    both = jnp.concatenate([back_re, back_im], axis=0)
    return jnp.einsum("nk,kml->nml", inv_a, both, precision=full_precision)


def spectral_block(signals, taps):
    seq_length, lanes = signals.shape
    tables = spectral_tables(seq_length)
    inner = tables[2].shape[2]
    rows = seq_length // inner
    half_lanes = lanes // 2
    sig_re, sig_im = forward_spectrum(signals.reshape(rows, inner, lanes), tables)
    taps_re, taps_im = forward_spectrum(taps.reshape(rows, inner, lanes), tables)
    lane = lax.broadcasted_iota(jnp.int32, (1, 1, lanes), 2)
    taps_im = jnp.where(lane < half_lanes, taps_im, -taps_im)
    pair_re = sig_re * taps_re - sig_im * taps_im
    pair_im = sig_re * taps_im + sig_im * taps_re
    turned_re = jnp.roll(sig_re, half_lanes, axis=2)
    turned_im = jnp.roll(sig_im, half_lanes, axis=2)
    cross_re = sig_re * turned_re + sig_im * turned_im
    cross_im = sig_re * turned_im - sig_im * turned_re
    pair = inverse_spectrum(pair_re, pair_im, tables).reshape(seq_length, lanes)
    cross = inverse_spectrum(cross_re, cross_im, tables).reshape(seq_length, lanes)
    return pair, cross


def on_device(query_proj, key_proj, value_proj, cotangent, long_filter, skip_gain):
    query_rows = query_proj[0].astype(jnp.float32)
    key_rows = key_proj[0].astype(jnp.float32)
    value_rows = value_proj[0].astype(jnp.float32)
    cot_rows = cotangent[0].astype(jnp.float32)
    local_length, chan_width = query_proj.shape[1], query_proj.shape[2]
    seq_count = lax.axis_size("seq")
    batch_count = lax.axis_size("dp")
    groups = seq_count * batch_count
    share = chan_width // groups
    seq_length = seq_count * local_length
    factor = (batch_count * seq_length) ** (-0.5)
    mixed = (key_rows * value_rows).astype(jnp.bfloat16)
    weighted = (cot_rows * query_rows).astype(jnp.bfloat16)

    mixed_wide = mixed.astype(jnp.float32)
    weighted_wide = weighted.astype(jnp.float32)
    gain_part = jnp.sum(weighted_wide * mixed_wide, axis=0)
    total = gain_part
    distance = 1
    while distance < groups:
        partners = [(i, i ^ distance) for i in range(groups)]
        total = total + lax.ppermute(total, ("seq", "dp"), partners)
        distance *= 2
    grad_skip = factor * total

    pair = jnp.stack([mixed.T, weighted.T], axis=0).reshape(2, groups, share, local_length)
    pair = jnp.transpose(pair, (1, 0, 2, 3)).reshape(groups, 2 * share, local_length)
    half_length = local_length // batch_count
    taps_t = long_filter.T.reshape(groups, share, batch_count, half_length)
    taps_mine = lax.dynamic_index_in_dim(taps_t, lax.axis_index("dp"), axis=2, keepdims=False)
    taps_rows = share * half_length // local_length
    taps_mine = taps_mine.astype(jnp.bfloat16).reshape(groups, taps_rows, local_length)
    send = jnp.concatenate([pair, taps_mine], axis=1)
    got = lax.all_to_all(send, ("seq", "dp"), 0, 0, tiled=True)

    pair_t = got[:, : 2 * share].reshape(seq_count, batch_count, 2, share, local_length)
    signals = jnp.transpose(pair_t, (0, 4, 2, 1, 3)).reshape(seq_length, 2 * batch_count * share)
    taps_t = got[:, 2 * share :].reshape(seq_count, batch_count, share, half_length)
    taps = jnp.transpose(taps_t, (0, 1, 3, 2)).reshape(seq_length, 1, share)
    taps = jnp.broadcast_to(taps, (seq_length, 2 * batch_count, share)).reshape(
        seq_length, 2 * batch_count * share
    )

    pair_vals, cross = spectral_block(signals.astype(jnp.float32), taps.astype(jnp.float32))
    pair_vals = pair_vals.reshape(seq_length, 2, batch_count, share)
    cross = cross.reshape(seq_length, 2, batch_count, share)
    slope = jnp.sum(cross[:, 0], axis=1)

    pair_back = pair_vals.astype(jnp.bfloat16).reshape(
        seq_count, local_length, 2, batch_count, share
    )
    pair_back = jnp.transpose(pair_back, (0, 3, 2, 4, 1)).reshape(
        groups, 2 * share, local_length
    )
    slope_blocks = jnp.swapaxes(slope.astype(jnp.bfloat16).reshape(seq_count, local_length, share), 1, 2)
    slope_send = jnp.broadcast_to(
        slope_blocks[:, None], (seq_count, batch_count, share, local_length)
    ).reshape(groups, share, local_length)
    home = lax.all_to_all(
        jnp.concatenate([pair_back, slope_send], axis=1), ("seq", "dp"), 0, 0, tiled=True
    )
    pair_home = home[:, : 2 * share].reshape(groups, 2, share, local_length)
    pair_home = jnp.transpose(pair_home, (1, 0, 2, 3)).reshape(2, chan_width, local_length)
    conv_rows = pair_home[0].T.astype(jnp.float32)
    corr_rows = pair_home[1].T.astype(jnp.float32)
    slope_home = home[:, 2 * share :].reshape(chan_width, local_length)
    grad_filter = factor * slope_home.T.astype(jnp.float32)

    signal = conv_rows + skip_gain[None, :] * mixed_wide
    output = (query_rows * signal).astype(jnp.bfloat16)
    grad_query = (cot_rows * signal).astype(jnp.bfloat16)
    back = corr_rows + skip_gain[None, :] * weighted_wide
    grad_key = (back * value_rows).astype(jnp.bfloat16)
    grad_value = (back * key_rows).astype(jnp.bfloat16)
    return (
        output[None],
        grad_query[None],
        grad_key[None],
        grad_value[None],
        grad_filter,
        grad_skip,
    )


def solution(mesh):
    return jax.shard_map(
        on_device,
        mesh=mesh,
        in_specs=(
            P("dp", "seq", "chan"),
            P("dp", "seq", "chan"),
            P("dp", "seq", "chan"),
            P("dp", "seq", "chan"),
            P("seq", "chan"),
            P("chan"),
        ),
        out_specs=(
            P("dp", "seq", "chan"),
            P("dp", "seq", "chan"),
            P("dp", "seq", "chan"),
            P("dp", "seq", "chan"),
            P("seq", "chan"),
            P("chan"),
        ),
        check_vma=False,
    )
```

```python
import math

import jax
import jax.numpy as jnp
from jax import lax
from jax.sharding import PartitionSpec as P

full_precision = lax.Precision.HIGHEST


def spectral_tables(seq_length):
    full_size = 2 * seq_length
    inner = 128
    outer = full_size // inner
    rows = seq_length // inner
    half = outer // 2 + 1
    k_index = jnp.arange(half, dtype=jnp.int32)
    n_index = jnp.arange(rows, dtype=jnp.int32)
    m_index = jnp.arange(inner, dtype=jnp.int32)
    j_index = jnp.arange(inner, dtype=jnp.int32)
    first_angle = (2.0 * math.pi / outer) * (
        (k_index[:, None] * n_index[None, :]) % outer
    ).astype(jnp.float32)
    first_cos = jnp.cos(first_angle)
    first_sin = jnp.sin(first_angle)
    stage_a = jnp.concatenate([first_cos, -first_sin], axis=0)
    weight = jnp.where((k_index == 0) | (k_index == outer // 2), 1.0, 2.0) / full_size
    inv_a = jnp.concatenate(
        [(first_cos * weight[:, None]).T, (-first_sin * weight[:, None]).T], axis=1
    )
    twist_angle = (2.0 * math.pi / full_size) * (
        (k_index[:, None] * m_index[None, :]) % full_size
    ).astype(jnp.float32)
    twist_cos, twist_sin = jnp.cos(twist_angle), jnp.sin(twist_angle)
    last_angle = (2.0 * math.pi / inner) * (
        (j_index[:, None] * m_index[None, :]) % inner
    ).astype(jnp.float32)
    last_cos, last_sin = jnp.cos(last_angle), jnp.sin(last_angle)
    g_re = twist_cos[:, None, :] * last_cos[None] - twist_sin[:, None, :] * last_sin[None]
    g_im = -(twist_sin[:, None, :] * last_cos[None] + twist_cos[:, None, :] * last_sin[None])
    fwd_table = jnp.concatenate([g_re, g_im], axis=1).astype(jnp.bfloat16)
    g_re_t = jnp.swapaxes(g_re, 1, 2)
    g_im_t = jnp.swapaxes(g_im, 1, 2)
    inv_table = jnp.concatenate([g_re_t, -g_im_t], axis=1).astype(jnp.bfloat16)
    return stage_a, inv_a, fwd_table, inv_table


def complex_stage(table, real_part, imag_part):
    inner = real_part.shape[1]
    a = jnp.einsum(
        "kjm,kml->kjl", table, real_part.astype(jnp.bfloat16),
        preferred_element_type=jnp.float32,
    )
    b = jnp.einsum(
        "kjm,kml->kjl", table, imag_part.astype(jnp.bfloat16),
        preferred_element_type=jnp.float32,
    )
    out_real = a[:, :inner] - b[:, inner:]
    out_imag = b[:, :inner] + a[:, inner:]
    return out_real, out_imag


def forward_spectrum(slab, tables):
    stage_a, _, fwd_table, _ = tables
    half = fwd_table.shape[0]
    first = jnp.einsum("kn,nml->kml", stage_a, slab, precision=full_precision)
    return complex_stage(fwd_table, first[:half], first[half:])


def inverse_spectrum(prod_re, prod_im, tables):
    _, inv_a, _, inv_table = tables
    back_re, back_im = complex_stage(inv_table, prod_re, prod_im)
    both = jnp.concatenate([back_re, back_im], axis=0)
    return jnp.einsum("nk,kml->nml", inv_a, both, precision=full_precision)


def spectral_block(signals, taps, carry):
    seq_length, lanes = signals.shape
    tables = spectral_tables(seq_length)
    inner = tables[2].shape[2]
    rows = seq_length // inner
    half_lanes = lanes // 2
    sig_re, sig_im = forward_spectrum(signals.reshape(rows, inner, lanes), tables)
    taps_re, taps_im = forward_spectrum(taps.reshape(rows, inner, lanes), tables)
    lane = lax.broadcasted_iota(jnp.int32, (1, 1, lanes), 2)
    taps_im = jnp.where(lane < half_lanes, taps_im, -taps_im)
    pair_re = sig_re * taps_re - sig_im * taps_im
    pair_im = sig_re * taps_im + sig_im * taps_re
    turned_re = jnp.roll(sig_re, half_lanes, axis=2)
    turned_im = jnp.roll(sig_im, half_lanes, axis=2)
    cross_re = sig_re * turned_re + sig_im * turned_im
    cross_im = sig_re * turned_im - sig_im * turned_re
    carry, pair_re, pair_im, cross_re, cross_im = lax.optimization_barrier(
        (carry, pair_re, pair_im, cross_re, cross_im)
    )
    pair = inverse_spectrum(pair_re, pair_im, tables).reshape(seq_length, lanes)
    cross = inverse_spectrum(cross_re, cross_im, tables).reshape(seq_length, lanes)
    return pair, cross, carry


def on_device(query_proj, key_proj, value_proj, cotangent, long_filter, skip_gain):
    query_rows = query_proj[0].astype(jnp.float32)
    key_rows = key_proj[0].astype(jnp.float32)
    value_rows = value_proj[0].astype(jnp.float32)
    cot_rows = cotangent[0].astype(jnp.float32)
    local_length, chan_width = query_proj.shape[1], query_proj.shape[2]
    seq_count = lax.axis_size("seq")
    batch_count = lax.axis_size("dp")
    groups = seq_count * batch_count
    share = chan_width // groups
    seq_length = seq_count * local_length
    factor = (batch_count * seq_length) ** (-0.5)
    mixed = (key_rows * value_rows).astype(jnp.bfloat16)
    weighted = (cot_rows * query_rows).astype(jnp.bfloat16)

    mixed_wide = mixed.astype(jnp.float32)
    weighted_wide = weighted.astype(jnp.float32)
    gain_part = jnp.sum(weighted_wide * mixed_wide, axis=0)

    pair = jnp.stack([mixed.T, weighted.T], axis=0).reshape(2, groups, share, local_length)
    pair = jnp.transpose(pair, (1, 0, 2, 3)).reshape(groups, 2 * share, local_length)
    half_length = local_length // batch_count
    taps_t = long_filter.T.reshape(groups, share, batch_count, half_length)
    taps_mine = lax.dynamic_index_in_dim(taps_t, lax.axis_index("dp"), axis=2, keepdims=False)
    taps_rows = share * half_length // local_length
    taps_mine = taps_mine.astype(jnp.bfloat16).reshape(groups, taps_rows, local_length)
    send = jnp.concatenate([pair, taps_mine], axis=1)
    got = lax.all_to_all(send, ("seq", "dp"), 0, 0, tiled=True)
    gain_part, got = lax.optimization_barrier((gain_part, got))
    total = gain_part
    distance = 1
    while distance < groups:
        partners = [(i, i ^ distance) for i in range(groups)]
        total = total + lax.ppermute(total, ("seq", "dp"), partners)
        distance *= 2
    grad_skip = factor * total

    pair_t = got[:, : 2 * share].reshape(seq_count, batch_count, 2, share, local_length)
    signals = jnp.transpose(pair_t, (0, 4, 2, 1, 3)).reshape(seq_length, 2 * batch_count * share)
    taps_t = got[:, 2 * share :].reshape(seq_count, batch_count, share, half_length)
    taps = jnp.transpose(taps_t, (0, 1, 3, 2)).reshape(seq_length, 1, share)
    taps = jnp.broadcast_to(taps, (seq_length, 2 * batch_count, share)).reshape(
        seq_length, 2 * batch_count * share
    )

    pair_vals, cross, grad_skip = spectral_block(
        signals.astype(jnp.float32), taps.astype(jnp.float32), grad_skip
    )
    pair_vals = pair_vals.reshape(seq_length, 2, batch_count, share)
    cross = cross.reshape(seq_length, 2, batch_count, share)
    slope = jnp.sum(cross[:, 0], axis=1)

    pair_back = pair_vals.astype(jnp.bfloat16).reshape(
        seq_count, local_length, 2, batch_count, share
    )
    pair_back = jnp.transpose(pair_back, (0, 3, 2, 4, 1)).reshape(
        groups, 2 * share, local_length
    )
    slope_blocks = jnp.swapaxes(slope.astype(jnp.bfloat16).reshape(seq_count, local_length, share), 1, 2)
    slope_send = jnp.broadcast_to(
        slope_blocks[:, None], (seq_count, batch_count, share, local_length)
    ).reshape(groups, share, local_length)
    home = lax.all_to_all(
        jnp.concatenate([pair_back, slope_send], axis=1), ("seq", "dp"), 0, 0, tiled=True
    )
    pair_home = home[:, : 2 * share].reshape(groups, 2, share, local_length)
    pair_home = jnp.transpose(pair_home, (1, 0, 2, 3)).reshape(2, chan_width, local_length)
    conv_rows = pair_home[0].T.astype(jnp.float32)
    corr_rows = pair_home[1].T.astype(jnp.float32)
    slope_home = home[:, 2 * share :].reshape(chan_width, local_length)
    grad_filter = factor * slope_home.T.astype(jnp.float32)

    signal = conv_rows + skip_gain[None, :] * mixed_wide
    output = (query_rows * signal).astype(jnp.bfloat16)
    grad_query = (cot_rows * signal).astype(jnp.bfloat16)
    back = corr_rows + skip_gain[None, :] * weighted_wide
    grad_key = (back * value_rows).astype(jnp.bfloat16)
    grad_value = (back * key_rows).astype(jnp.bfloat16)
    return (
        output[None],
        grad_query[None],
        grad_key[None],
        grad_value[None],
        grad_filter,
        grad_skip,
    )


def solution(mesh):
    return jax.shard_map(
        on_device,
        mesh=mesh,
        in_specs=(
            P("dp", "seq", "chan"),
            P("dp", "seq", "chan"),
            P("dp", "seq", "chan"),
            P("dp", "seq", "chan"),
            P("seq", "chan"),
            P("chan"),
        ),
        out_specs=(
            P("dp", "seq", "chan"),
            P("dp", "seq", "chan"),
            P("dp", "seq", "chan"),
            P("dp", "seq", "chan"),
            P("seq", "chan"),
            P("chan"),
        ),
        check_vma=False,
    )
```

```python
import math

import jax
import jax.numpy as jnp
from jax import lax
from jax.sharding import PartitionSpec as P

full_precision = lax.Precision.HIGHEST


def spectral_tables(seq_length):
    full_size = 2 * seq_length
    inner = 128
    outer = full_size // inner
    rows = seq_length // inner
    half = outer // 2 + 1
    k_index = jnp.arange(half, dtype=jnp.int32)
    n_index = jnp.arange(rows, dtype=jnp.int32)
    m_index = jnp.arange(inner, dtype=jnp.int32)
    j_index = jnp.arange(inner, dtype=jnp.int32)
    first_angle = (2.0 * math.pi / outer) * (
        (k_index[:, None] * n_index[None, :]) % outer
    ).astype(jnp.float32)
    first_cos = jnp.cos(first_angle)
    first_sin = jnp.sin(first_angle)
    stage_a = jnp.concatenate([first_cos, -first_sin], axis=0)
    weight = jnp.where((k_index == 0) | (k_index == outer // 2), 1.0, 2.0) / full_size
    inv_a = jnp.concatenate(
        [(first_cos * weight[:, None]).T, (-first_sin * weight[:, None]).T], axis=1
    )
    twist_angle = (2.0 * math.pi / full_size) * (
        (k_index[:, None] * m_index[None, :]) % full_size
    ).astype(jnp.float32)
    twist_cos, twist_sin = jnp.cos(twist_angle), jnp.sin(twist_angle)
    last_angle = (2.0 * math.pi / inner) * (
        (j_index[:, None] * m_index[None, :]) % inner
    ).astype(jnp.float32)
    last_cos, last_sin = jnp.cos(last_angle), jnp.sin(last_angle)
    g_re = twist_cos[:, None, :] * last_cos[None] - twist_sin[:, None, :] * last_sin[None]
    g_im = -(twist_sin[:, None, :] * last_cos[None] + twist_cos[:, None, :] * last_sin[None])
    fwd_table = jnp.concatenate([g_re, g_im], axis=1).astype(jnp.bfloat16)
    g_re_t = jnp.swapaxes(g_re, 1, 2)
    g_im_t = jnp.swapaxes(g_im, 1, 2)
    inv_table = jnp.concatenate([g_re_t, -g_im_t], axis=1).astype(jnp.bfloat16)
    return stage_a, inv_a, fwd_table, inv_table


def complex_stage(table, real_part, imag_part):
    inner = real_part.shape[1]
    a = jnp.einsum(
        "kjm,kml->kjl", table, real_part.astype(jnp.bfloat16),
        preferred_element_type=jnp.float32,
    )
    b = jnp.einsum(
        "kjm,kml->kjl", table, imag_part.astype(jnp.bfloat16),
        preferred_element_type=jnp.float32,
    )
    out_real = a[:, :inner] - b[:, inner:]
    out_imag = b[:, :inner] + a[:, inner:]
    return out_real, out_imag


def forward_spectrum(slab, tables):
    stage_a, _, fwd_table, _ = tables
    half = fwd_table.shape[0]
    first = jnp.einsum("kn,nml->kml", stage_a, slab, precision=full_precision)
    return complex_stage(fwd_table, first[:half], first[half:])


def inverse_spectrum(prod_re, prod_im, tables):
    _, inv_a, _, inv_table = tables
    back_re, back_im = complex_stage(inv_table, prod_re, prod_im)
    both = jnp.concatenate([back_re, back_im], axis=0)
    return jnp.einsum("nk,kml->nml", inv_a, both, precision=full_precision)


def spectral_products(signals, taps, carry):
    seq_length, lanes = signals.shape
    tables = spectral_tables(seq_length)
    inner = tables[2].shape[2]
    rows = seq_length // inner
    half_lanes = lanes // 2
    taps_re, taps_im = forward_spectrum(taps.reshape(rows, inner, lanes), tables)
    sig_re, sig_im = forward_spectrum(signals.reshape(rows, inner, lanes), tables)
    lane = lax.broadcasted_iota(jnp.int32, (1, 1, lanes), 2)
    taps_im = jnp.where(lane < half_lanes, taps_im, -taps_im)
    pair_re = sig_re * taps_re - sig_im * taps_im
    pair_im = sig_re * taps_im + sig_im * taps_re
    turned_re = jnp.roll(sig_re, half_lanes, axis=2)
    turned_im = jnp.roll(sig_im, half_lanes, axis=2)
    cross_re = sig_re * turned_re + sig_im * turned_im
    cross_im = sig_re * turned_im - sig_im * turned_re
    carry, pair_re, pair_im, cross_re, cross_im = lax.optimization_barrier(
        (carry, pair_re, pair_im, cross_re, cross_im)
    )
    return tables, (pair_re, pair_im), (cross_re, cross_im), carry


def on_device(query_proj, key_proj, value_proj, cotangent, long_filter, skip_gain):
    query_rows = query_proj[0].astype(jnp.float32)
    key_rows = key_proj[0].astype(jnp.float32)
    value_rows = value_proj[0].astype(jnp.float32)
    cot_rows = cotangent[0].astype(jnp.float32)
    local_length, chan_width = query_proj.shape[1], query_proj.shape[2]
    seq_count = lax.axis_size("seq")
    batch_count = lax.axis_size("dp")
    groups = seq_count * batch_count
    share = chan_width // groups
    seq_length = seq_count * local_length
    factor = (batch_count * seq_length) ** (-0.5)
    mixed = (key_rows * value_rows).astype(jnp.bfloat16)
    weighted = (cot_rows * query_rows).astype(jnp.bfloat16)

    mixed_wide = mixed.astype(jnp.float32)
    weighted_wide = weighted.astype(jnp.float32)
    gain_part = jnp.sum(weighted_wide * mixed_wide, axis=0)

    pair = jnp.stack([mixed.T, weighted.T], axis=0).reshape(2, groups, share, local_length)
    pair = jnp.transpose(pair, (1, 0, 2, 3)).reshape(groups, 2 * share, local_length)
    half_length = local_length // batch_count
    taps_t = long_filter.T.reshape(groups, share, batch_count, half_length)
    taps_mine = lax.dynamic_index_in_dim(taps_t, lax.axis_index("dp"), axis=2, keepdims=False)
    taps_rows = share * half_length // local_length
    taps_mine = taps_mine.astype(jnp.bfloat16).reshape(groups, taps_rows, local_length)
    taps_got = lax.all_to_all(taps_mine, ("seq", "dp"), 0, 0, tiled=True)
    got = lax.all_to_all(pair, ("seq", "dp"), 0, 0, tiled=True)
    gain_part, got = lax.optimization_barrier((gain_part, got))
    total = gain_part
    distance = 1
    while distance < groups:
        partners = [(i, i ^ distance) for i in range(groups)]
        total = total + lax.ppermute(total, ("seq", "dp"), partners)
        distance *= 2
    grad_skip = factor * total

    pair_t = got.reshape(seq_count, batch_count, 2, share, local_length)
    signals = jnp.transpose(pair_t, (0, 4, 2, 1, 3)).reshape(seq_length, 2 * batch_count * share)
    taps_t = taps_got.reshape(seq_count, batch_count, share, half_length)
    taps = jnp.transpose(taps_t, (0, 1, 3, 2)).reshape(seq_length, 1, share)
    taps = jnp.broadcast_to(taps, (seq_length, 2 * batch_count, share)).reshape(
        seq_length, 2 * batch_count * share
    )

    tables, pair_spec, cross_spec, grad_skip = spectral_products(
        signals.astype(jnp.float32), taps.astype(jnp.float32), grad_skip
    )
    pair_vals = inverse_spectrum(pair_spec[0], pair_spec[1], tables)
    pair_vals = pair_vals.reshape(seq_length, 2, batch_count, share)

    pair_back = pair_vals.astype(jnp.bfloat16).reshape(
        seq_count, local_length, 2, batch_count, share
    )
    pair_back = jnp.transpose(pair_back, (0, 3, 2, 4, 1)).reshape(
        groups, 2 * share, local_length
    )
    pair_home = lax.all_to_all(pair_back, ("seq", "dp"), 0, 0, tiled=True)

    cross = inverse_spectrum(cross_spec[0], cross_spec[1], tables)
    cross = cross.reshape(seq_length, 2, batch_count, share)
    slope = jnp.sum(cross[:, 0], axis=1)
    slope_blocks = jnp.swapaxes(slope.astype(jnp.bfloat16).reshape(seq_count, local_length, share), 1, 2)
    slope_send = jnp.broadcast_to(
        slope_blocks[:, None], (seq_count, batch_count, share, local_length)
    ).reshape(groups, share, local_length)
    slope_home = lax.all_to_all(slope_send, ("seq", "dp"), 0, 0, tiled=True)

    pair_home = pair_home.reshape(groups, 2, share, local_length)
    pair_home = jnp.transpose(pair_home, (1, 0, 2, 3)).reshape(2, chan_width, local_length)
    conv_rows = pair_home[0].T.astype(jnp.float32)
    corr_rows = pair_home[1].T.astype(jnp.float32)
    grad_filter = factor * slope_home.reshape(chan_width, local_length).T.astype(jnp.float32)

    signal = conv_rows + skip_gain[None, :] * mixed_wide
    output = (query_rows * signal).astype(jnp.bfloat16)
    grad_query = (cot_rows * signal).astype(jnp.bfloat16)
    back = corr_rows + skip_gain[None, :] * weighted_wide
    grad_key = (back * value_rows).astype(jnp.bfloat16)
    grad_value = (back * key_rows).astype(jnp.bfloat16)
    return (
        output[None],
        grad_query[None],
        grad_key[None],
        grad_value[None],
        grad_filter,
        grad_skip,
    )


def solution(mesh):
    return jax.shard_map(
        on_device,
        mesh=mesh,
        in_specs=(
            P("dp", "seq", "chan"),
            P("dp", "seq", "chan"),
            P("dp", "seq", "chan"),
            P("dp", "seq", "chan"),
            P("seq", "chan"),
            P("chan"),
        ),
        out_specs=(
            P("dp", "seq", "chan"),
            P("dp", "seq", "chan"),
            P("dp", "seq", "chan"),
            P("dp", "seq", "chan"),
            P("seq", "chan"),
            P("chan"),
        ),
        check_vma=False,
    )
```

```python
import math

import jax
import jax.numpy as jnp
from jax import lax
from jax.experimental import pallas as pl
from jax.experimental.pallas import tpu as pltpu
from jax.sharding import PartitionSpec as P

full_precision = lax.Precision.HIGHEST


def spectral_tables(seq_length):
    full_size = 2 * seq_length
    inner = 128
    outer = full_size // inner
    rows = seq_length // inner
    half = outer // 2 + 1
    k_index = jnp.arange(half, dtype=jnp.int32)
    n_index = jnp.arange(rows, dtype=jnp.int32)
    m_index = jnp.arange(inner, dtype=jnp.int32)
    j_index = jnp.arange(inner, dtype=jnp.int32)
    first_angle = (2.0 * math.pi / outer) * (
        (k_index[:, None] * n_index[None, :]) % outer
    ).astype(jnp.float32)
    first_cos = jnp.cos(first_angle)
    first_sin = jnp.sin(first_angle)
    stage_a = jnp.concatenate([first_cos, -first_sin], axis=0)
    weight = jnp.where((k_index == 0) | (k_index == outer // 2), 1.0, 2.0) / full_size
    inv_a = jnp.concatenate(
        [(first_cos * weight[:, None]).T, (-first_sin * weight[:, None]).T], axis=1
    )
    twist_angle = (2.0 * math.pi / full_size) * (
        (k_index[:, None] * m_index[None, :]) % full_size
    ).astype(jnp.float32)
    twist_cos, twist_sin = jnp.cos(twist_angle), jnp.sin(twist_angle)
    last_angle = (2.0 * math.pi / inner) * (
        (j_index[:, None] * m_index[None, :]) % inner
    ).astype(jnp.float32)
    last_cos, last_sin = jnp.cos(last_angle), jnp.sin(last_angle)
    g_re = twist_cos[:, None, :] * last_cos[None] - twist_sin[:, None, :] * last_sin[None]
    g_im = -(twist_sin[:, None, :] * last_cos[None] + twist_cos[:, None, :] * last_sin[None])
    fwd_table = jnp.concatenate([g_re, g_im], axis=1).astype(jnp.bfloat16)
    g_re_t = jnp.swapaxes(g_re, 1, 2)
    g_im_t = jnp.swapaxes(g_im, 1, 2)
    inv_table = jnp.concatenate([g_re_t, -g_im_t], axis=1).astype(jnp.bfloat16)
    return stage_a, inv_a, fwd_table, inv_table


def complex_stage(table, real_part, imag_part):
    inner = real_part.shape[1]
    a = jnp.einsum(
        "kjm,kml->kjl", table, real_part.astype(jnp.bfloat16),
        preferred_element_type=jnp.float32,
    )
    b = jnp.einsum(
        "kjm,kml->kjl", table, imag_part.astype(jnp.bfloat16),
        preferred_element_type=jnp.float32,
    )
    out_real = a[:, :inner] - b[:, inner:]
    out_imag = b[:, :inner] + a[:, inner:]
    return out_real, out_imag


def forward_spectrum(slab, tables):
    stage_a, _, fwd_table, _ = tables
    half = fwd_table.shape[0]
    first = jnp.einsum("kn,nml->kml", stage_a, slab, precision=full_precision)
    return complex_stage(fwd_table, first[:half], first[half:])


def inverse_spectrum(prod_re, prod_im, tables):
    _, inv_a, _, inv_table = tables
    back_re, back_im = complex_stage(inv_table, prod_re, prod_im)
    both = jnp.concatenate([back_re, back_im], axis=0)
    return jnp.einsum("nk,kml->nml", inv_a, both, precision=full_precision)


def middle_kernel(
    sig_re_ref, sig_im_ref, taps_re_ref, taps_im_ref, fwd_ref, inv_ref,
    pair_re_ref, pair_im_ref, cross_re_ref, cross_im_ref,
):
    inner = sig_re_ref.shape[1]
    lanes = sig_re_ref.shape[2]
    half_lanes = lanes // 2
    fwd = fwd_ref[0]
    inv = inv_ref[0]

    def stage(table, real_part, imag_part):
        a = jnp.dot(table, real_part.astype(jnp.bfloat16), preferred_element_type=jnp.float32)
        b = jnp.dot(table, imag_part.astype(jnp.bfloat16), preferred_element_type=jnp.float32)
        return a[:inner] - b[inner:], b[:inner] + a[inner:]

    sig_re, sig_im = stage(fwd, sig_re_ref[0], sig_im_ref[0])
    taps_re, taps_im = stage(fwd, taps_re_ref[0], taps_im_ref[0])
    lane = lax.broadcasted_iota(jnp.int32, (inner, lanes), 1)
    taps_im = jnp.where(lane < half_lanes, taps_im, -taps_im)
    prod_re = sig_re * taps_re - sig_im * taps_im
    prod_im = sig_re * taps_im + sig_im * taps_re
    out_re, out_im = stage(inv, prod_re, prod_im)
    pair_re_ref[0] = out_re
    pair_im_ref[0] = out_im
    turned_re = pltpu.roll(sig_re, half_lanes, 1)
    turned_im = pltpu.roll(sig_im, half_lanes, 1)
    prod_re = sig_re * turned_re + sig_im * turned_im
    prod_im = sig_re * turned_im - sig_im * turned_re
    out_re, out_im = stage(inv, prod_re, prod_im)
    cross_re_ref[0] = out_re
    cross_im_ref[0] = out_im


def spectral_middle(sig_first, taps_first, fwd_table, inv_table):
    half, rows2, inner = fwd_table.shape
    lanes = sig_first.shape[2]
    block = pl.BlockSpec((1, inner, lanes), lambda k: (k, 0, 0))
    block_im = pl.BlockSpec((1, inner, lanes), lambda k: (k + half, 0, 0))
    table_block = pl.BlockSpec((1, rows2, inner), lambda k: (k, 0, 0))
    out_shape = jax.ShapeDtypeStruct((half, inner, lanes), jnp.float32)
    flops = half * 6 * 2 * 2 * rows2 * inner * lanes
    bytes_accessed = half * (8 * inner * lanes * 4 + 2 * rows2 * inner * 2)
    return pl.pallas_call(
        middle_kernel,
        grid=(half,),
        in_specs=[block, block_im, block, block_im, table_block, table_block],
        out_specs=[block] * 4,
        out_shape=[out_shape] * 4,
        cost_estimate=pl.CostEstimate(
            flops=flops, transcendentals=0, bytes_accessed=bytes_accessed
        ),
    )(sig_first, sig_first, taps_first, taps_first, fwd_table, inv_table)


def spectral_products(signals, taps, carry):
    seq_length, lanes = signals.shape
    tables = spectral_tables(seq_length)
    stage_a, _, fwd_table, inv_table = tables
    inner = fwd_table.shape[2]
    rows = seq_length // inner
    taps_first = jnp.einsum(
        "kn,nml->kml", stage_a, taps.reshape(rows, inner, lanes), precision=full_precision
    )
    sig_first = jnp.einsum(
        "kn,nml->kml", stage_a, signals.reshape(rows, inner, lanes), precision=full_precision
    )
    pair_re, pair_im, cross_re, cross_im = spectral_middle(
        sig_first, taps_first, fwd_table, inv_table
    )
    carry, pair_re, pair_im, cross_re, cross_im = lax.optimization_barrier(
        (carry, pair_re, pair_im, cross_re, cross_im)
    )
    return tables, (pair_re, pair_im), (cross_re, cross_im), carry


def spectral_inverse(back_re, back_im, tables):
    inv_a = tables[1]
    both = jnp.concatenate([back_re, back_im], axis=0)
    return jnp.einsum("nk,kml->nml", inv_a, both, precision=full_precision)


def on_device(query_proj, key_proj, value_proj, cotangent, long_filter, skip_gain):
    query_rows = query_proj[0].astype(jnp.float32)
    key_rows = key_proj[0].astype(jnp.float32)
    value_rows = value_proj[0].astype(jnp.float32)
    cot_rows = cotangent[0].astype(jnp.float32)
    local_length, chan_width = query_proj.shape[1], query_proj.shape[2]
    seq_count = lax.axis_size("seq")
    batch_count = lax.axis_size("dp")
    groups = seq_count * batch_count
    share = chan_width // groups
    seq_length = seq_count * local_length
    factor = (batch_count * seq_length) ** (-0.5)
    mixed = (key_rows * value_rows).astype(jnp.bfloat16)
    weighted = (cot_rows * query_rows).astype(jnp.bfloat16)

    mixed_wide = mixed.astype(jnp.float32)
    weighted_wide = weighted.astype(jnp.float32)
    gain_part = jnp.sum(weighted_wide * mixed_wide, axis=0)

    pair = jnp.stack([mixed.T, weighted.T], axis=0).reshape(2, groups, share, local_length)
    pair = jnp.transpose(pair, (1, 0, 2, 3)).reshape(groups, 2 * share, local_length)
    half_length = local_length // batch_count
    taps_t = long_filter.T.reshape(groups, share, batch_count, half_length)
    taps_mine = lax.dynamic_index_in_dim(taps_t, lax.axis_index("dp"), axis=2, keepdims=False)
    taps_rows = share * half_length // local_length
    taps_mine = taps_mine.astype(jnp.bfloat16).reshape(groups, taps_rows, local_length)
    taps_got = lax.all_to_all(taps_mine, ("seq", "dp"), 0, 0, tiled=True)
    got = lax.all_to_all(pair, ("seq", "dp"), 0, 0, tiled=True)
    gain_part, got = lax.optimization_barrier((gain_part, got))
    total = gain_part
    distance = 1
    while distance < groups:
        partners = [(i, i ^ distance) for i in range(groups)]
        total = total + lax.ppermute(total, ("seq", "dp"), partners)
        distance *= 2
    grad_skip = factor * total

    pair_t = got.reshape(seq_count, batch_count, 2, share, local_length)
    signals = jnp.transpose(pair_t, (0, 4, 2, 1, 3)).reshape(seq_length, 2 * batch_count * share)
    taps_t = taps_got.reshape(seq_count, batch_count, share, half_length)
    taps = jnp.transpose(taps_t, (0, 1, 3, 2)).reshape(seq_length, 1, share)
    taps = jnp.broadcast_to(taps, (seq_length, 2 * batch_count, share)).reshape(
        seq_length, 2 * batch_count * share
    )

    tables, pair_spec, cross_spec, grad_skip = spectral_products(
        signals.astype(jnp.float32), taps.astype(jnp.float32), grad_skip
    )
    pair_vals = spectral_inverse(pair_spec[0], pair_spec[1], tables)
    pair_vals = pair_vals.reshape(seq_length, 2, batch_count, share)

    pair_back = pair_vals.astype(jnp.bfloat16).reshape(
        seq_count, local_length, 2, batch_count, share
    )
    pair_back = jnp.transpose(pair_back, (0, 3, 2, 4, 1)).reshape(
        groups, 2 * share, local_length
    )
    pair_home = lax.all_to_all(pair_back, ("seq", "dp"), 0, 0, tiled=True)

    cross = spectral_inverse(cross_spec[0], cross_spec[1], tables)
    cross = cross.reshape(seq_length, 2, batch_count, share)
    slope = jnp.sum(cross[:, 0], axis=1)
    slope_blocks = jnp.swapaxes(slope.astype(jnp.bfloat16).reshape(seq_count, local_length, share), 1, 2)
    slope_send = jnp.broadcast_to(
        slope_blocks[:, None], (seq_count, batch_count, share, local_length)
    ).reshape(groups, share, local_length)
    slope_home = lax.all_to_all(slope_send, ("seq", "dp"), 0, 0, tiled=True)

    pair_home = pair_home.reshape(groups, 2, share, local_length)
    pair_home = jnp.transpose(pair_home, (1, 0, 2, 3)).reshape(2, chan_width, local_length)
    conv_rows = pair_home[0].T.astype(jnp.float32)
    corr_rows = pair_home[1].T.astype(jnp.float32)
    grad_filter = factor * slope_home.reshape(chan_width, local_length).T.astype(jnp.float32)

    signal = conv_rows + skip_gain[None, :] * mixed_wide
    output = (query_rows * signal).astype(jnp.bfloat16)
    grad_query = (cot_rows * signal).astype(jnp.bfloat16)
    back = corr_rows + skip_gain[None, :] * weighted_wide
    grad_key = (back * value_rows).astype(jnp.bfloat16)
    grad_value = (back * key_rows).astype(jnp.bfloat16)
    return (
        output[None],
        grad_query[None],
        grad_key[None],
        grad_value[None],
        grad_filter,
        grad_skip,
    )


def solution(mesh):
    return jax.shard_map(
        on_device,
        mesh=mesh,
        in_specs=(
            P("dp", "seq", "chan"),
            P("dp", "seq", "chan"),
            P("dp", "seq", "chan"),
            P("dp", "seq", "chan"),
            P("seq", "chan"),
            P("chan"),
        ),
        out_specs=(
            P("dp", "seq", "chan"),
            P("dp", "seq", "chan"),
            P("dp", "seq", "chan"),
            P("dp", "seq", "chan"),
            P("seq", "chan"),
            P("chan"),
        ),
        check_vma=False,
    )
```

```python
import math

import jax
import jax.numpy as jnp
from jax import lax
from jax.experimental import pallas as pl
from jax.experimental.pallas import tpu as pltpu
from jax.sharding import PartitionSpec as P

full_precision = lax.Precision.HIGHEST


def spectral_tables(seq_length):
    full_size = 2 * seq_length
    inner = 128
    outer = full_size // inner
    rows = seq_length // inner
    half = outer // 2 + 1
    k_index = jnp.arange(half, dtype=jnp.int32)
    n_index = jnp.arange(rows, dtype=jnp.int32)
    m_index = jnp.arange(inner, dtype=jnp.int32)
    j_index = jnp.arange(inner, dtype=jnp.int32)
    first_angle = (2.0 * math.pi / outer) * (
        (k_index[:, None] * n_index[None, :]) % outer
    ).astype(jnp.float32)
    first_cos = jnp.cos(first_angle)
    first_sin = jnp.sin(first_angle)
    stage_a = jnp.concatenate([first_cos, -first_sin], axis=0)
    weight = jnp.where((k_index == 0) | (k_index == outer // 2), 1.0, 2.0) / full_size
    inv_a = jnp.concatenate(
        [(first_cos * weight[:, None]).T, (-first_sin * weight[:, None]).T], axis=1
    )
    twist_angle = (2.0 * math.pi / full_size) * (
        (k_index[:, None] * m_index[None, :]) % full_size
    ).astype(jnp.float32)
    twist_cos, twist_sin = jnp.cos(twist_angle), jnp.sin(twist_angle)
    last_angle = (2.0 * math.pi / inner) * (
        (j_index[:, None] * m_index[None, :]) % inner
    ).astype(jnp.float32)
    last_cos, last_sin = jnp.cos(last_angle), jnp.sin(last_angle)
    g_re = twist_cos[:, None, :] * last_cos[None] - twist_sin[:, None, :] * last_sin[None]
    g_im = -(twist_sin[:, None, :] * last_cos[None] + twist_cos[:, None, :] * last_sin[None])
    fwd_table = jnp.concatenate([g_re, g_im], axis=1).astype(jnp.bfloat16)
    g_re_t = jnp.swapaxes(g_re, 1, 2)
    g_im_t = jnp.swapaxes(g_im, 1, 2)
    inv_table = jnp.concatenate([g_re_t, -g_im_t], axis=1).astype(jnp.bfloat16)
    return stage_a, inv_a, fwd_table, inv_table


def complex_stage(table, real_part, imag_part):
    inner = real_part.shape[1]
    a = jnp.einsum(
        "kjm,kml->kjl", table, real_part.astype(jnp.bfloat16),
        preferred_element_type=jnp.float32,
    )
    b = jnp.einsum(
        "kjm,kml->kjl", table, imag_part.astype(jnp.bfloat16),
        preferred_element_type=jnp.float32,
    )
    out_real = a[:, :inner] - b[:, inner:]
    out_imag = b[:, :inner] + a[:, inner:]
    return out_real, out_imag


def forward_spectrum(slab, tables):
    stage_a, _, fwd_table, _ = tables
    half = fwd_table.shape[0]
    first = jnp.einsum("kn,nml->kml", stage_a, slab, precision=full_precision)
    return complex_stage(fwd_table, first[:half], first[half:])


def inverse_spectrum(prod_re, prod_im, tables):
    _, inv_a, _, inv_table = tables
    back_re, back_im = complex_stage(inv_table, prod_re, prod_im)
    both = jnp.concatenate([back_re, back_im], axis=0)
    return jnp.einsum("nk,kml->nml", inv_a, both, precision=full_precision)


def middle_kernel(
    sig_re_ref, sig_im_ref, taps_re_ref, taps_im_ref, fwd_ref, inv_ref,
    pair_re_ref, pair_im_ref, cross_re_ref, cross_im_ref,
):
    steps, inner, lanes = sig_re_ref.shape
    half_lanes = lanes // 2
    lane = lax.broadcasted_iota(jnp.int32, (inner, lanes), 1)
    for step in range(steps):
        first = jnp.concatenate(
            [sig_re_ref[step], sig_im_ref[step], taps_re_ref[step], taps_im_ref[step]], axis=1
        ).astype(jnp.bfloat16)
        spec = jnp.dot(fwd_ref[step], first, preferred_element_type=jnp.float32)
        sig_re = spec[:inner, 0:lanes] - spec[inner:, lanes : 2 * lanes]
        sig_im = spec[:inner, lanes : 2 * lanes] + spec[inner:, 0:lanes]
        taps_re = spec[:inner, 2 * lanes : 3 * lanes] - spec[inner:, 3 * lanes :]
        taps_im = spec[:inner, 3 * lanes :] + spec[inner:, 2 * lanes : 3 * lanes]
        taps_im = jnp.where(lane < half_lanes, taps_im, -taps_im)
        pair_re = sig_re * taps_re - sig_im * taps_im
        pair_im = sig_re * taps_im + sig_im * taps_re
        turned_re = pltpu.roll(sig_re, half_lanes, 1)
        turned_im = pltpu.roll(sig_im, half_lanes, 1)
        cross_re = sig_re * turned_re + sig_im * turned_im
        cross_im = sig_re * turned_im - sig_im * turned_re
        second = jnp.concatenate([pair_re, pair_im, cross_re, cross_im], axis=1).astype(
            jnp.bfloat16
        )
        back = jnp.dot(inv_ref[step], second, preferred_element_type=jnp.float32)
        pair_re_ref[step] = back[:inner, 0:lanes] - back[inner:, lanes : 2 * lanes]
        pair_im_ref[step] = back[:inner, lanes : 2 * lanes] + back[inner:, 0:lanes]
        cross_re_ref[step] = back[:inner, 2 * lanes : 3 * lanes] - back[inner:, 3 * lanes :]
        cross_im_ref[step] = back[:inner, 3 * lanes :] + back[inner:, 2 * lanes : 3 * lanes]


def spectral_middle(sig_first, taps_first, fwd_table, inv_table):
    half, rows2, inner = fwd_table.shape
    lanes = sig_first.shape[2]
    steps = 3 if half % 3 == 0 else 1
    count = half // steps
    block = pl.BlockSpec((steps, inner, lanes), lambda k: (k, 0, 0))
    block_im = pl.BlockSpec((steps, inner, lanes), lambda k: (k + count, 0, 0))
    table_block = pl.BlockSpec((steps, rows2, inner), lambda k: (k, 0, 0))
    out_shape = jax.ShapeDtypeStruct((half, inner, lanes), jnp.float32)
    flops = half * 2 * 2 * rows2 * inner * 4 * lanes
    bytes_accessed = half * (8 * inner * lanes * 4 + 2 * rows2 * inner * 2)
    return pl.pallas_call(
        middle_kernel,
        grid=(count,),
        in_specs=[block, block_im, block, block_im, table_block, table_block],
        out_specs=[block] * 4,
        out_shape=[out_shape] * 4,
        cost_estimate=pl.CostEstimate(
            flops=flops, transcendentals=0, bytes_accessed=bytes_accessed
        ),
    )(sig_first, sig_first, taps_first, taps_first, fwd_table, inv_table)


def spectral_products(signals, taps, carry):
    seq_length, lanes = signals.shape
    tables = spectral_tables(seq_length)
    stage_a, _, fwd_table, inv_table = tables
    inner = fwd_table.shape[2]
    rows = seq_length // inner
    taps_first = jnp.einsum(
        "kn,nml->kml", stage_a, taps.reshape(rows, inner, lanes), precision=full_precision
    )
    sig_first = jnp.einsum(
        "kn,nml->kml", stage_a, signals.reshape(rows, inner, lanes), precision=full_precision
    )
    pair_re, pair_im, cross_re, cross_im = spectral_middle(
        sig_first, taps_first, fwd_table, inv_table
    )
    carry, pair_re, pair_im, cross_re, cross_im = lax.optimization_barrier(
        (carry, pair_re, pair_im, cross_re, cross_im)
    )
    return tables, (pair_re, pair_im), (cross_re, cross_im), carry


def spectral_inverse(back_re, back_im, tables):
    inv_a = tables[1]
    both = jnp.concatenate([back_re, back_im], axis=0)
    return jnp.einsum("nk,kml->nml", inv_a, both, precision=full_precision)


def on_device(query_proj, key_proj, value_proj, cotangent, long_filter, skip_gain):
    query_rows = query_proj[0].astype(jnp.float32)
    key_rows = key_proj[0].astype(jnp.float32)
    value_rows = value_proj[0].astype(jnp.float32)
    cot_rows = cotangent[0].astype(jnp.float32)
    local_length, chan_width = query_proj.shape[1], query_proj.shape[2]
    seq_count = lax.axis_size("seq")
    batch_count = lax.axis_size("dp")
    groups = seq_count * batch_count
    share = chan_width // groups
    seq_length = seq_count * local_length
    factor = (batch_count * seq_length) ** (-0.5)
    mixed = (key_rows * value_rows).astype(jnp.bfloat16)
    weighted = (cot_rows * query_rows).astype(jnp.bfloat16)

    mixed_wide = mixed.astype(jnp.float32)
    weighted_wide = weighted.astype(jnp.float32)
    gain_part = jnp.sum(weighted_wide * mixed_wide, axis=0)

    pair = jnp.stack([mixed.T, weighted.T], axis=0).reshape(2, groups, share, local_length)
    pair = jnp.transpose(pair, (1, 0, 2, 3)).reshape(groups, 2 * share, local_length)
    half_length = local_length // batch_count
    taps_t = long_filter.T.reshape(groups, share, batch_count, half_length)
    taps_mine = lax.dynamic_index_in_dim(taps_t, lax.axis_index("dp"), axis=2, keepdims=False)
    taps_rows = share * half_length // local_length
    taps_mine = taps_mine.astype(jnp.bfloat16).reshape(groups, taps_rows, local_length)
    taps_got = lax.all_to_all(taps_mine, ("seq", "dp"), 0, 0, tiled=True)
    taps_got, pair = lax.optimization_barrier((taps_got, pair))
    got = lax.all_to_all(pair, ("seq", "dp"), 0, 0, tiled=True)
    gain_part, got = lax.optimization_barrier((gain_part, got))
    total = gain_part
    distance = 1
    while distance < groups:
        partners = [(i, i ^ distance) for i in range(groups)]
        total = total + lax.ppermute(total, ("seq", "dp"), partners)
        distance *= 2
    grad_skip = factor * total

    pair_t = got.reshape(seq_count, batch_count, 2, share, local_length)
    signals = jnp.transpose(pair_t, (0, 4, 2, 1, 3)).reshape(seq_length, 2 * batch_count * share)
    taps_t = taps_got.reshape(seq_count, batch_count, share, half_length)
    taps = jnp.transpose(taps_t, (0, 1, 3, 2)).reshape(seq_length, 1, share)
    taps = jnp.broadcast_to(taps, (seq_length, 2 * batch_count, share)).reshape(
        seq_length, 2 * batch_count * share
    )

    tables, pair_spec, cross_spec, grad_skip = spectral_products(
        signals.astype(jnp.float32), taps.astype(jnp.float32), grad_skip
    )
    pair_vals = spectral_inverse(pair_spec[0], pair_spec[1], tables)
    pair_vals = pair_vals.reshape(seq_length, 2, batch_count, share)

    pair_back = pair_vals.astype(jnp.bfloat16).reshape(
        seq_count, local_length, 2, batch_count, share
    )
    pair_back = jnp.transpose(pair_back, (0, 3, 2, 4, 1)).reshape(
        groups, 2 * share, local_length
    )
    pair_home = lax.all_to_all(pair_back, ("seq", "dp"), 0, 0, tiled=True)

    cross = spectral_inverse(cross_spec[0], cross_spec[1], tables)
    cross = cross.reshape(seq_length, 2, batch_count, share)
    slope = jnp.sum(cross[:, 0], axis=1)
    slope_blocks = jnp.swapaxes(slope.astype(jnp.bfloat16).reshape(seq_count, local_length, share), 1, 2)
    slope_send = jnp.broadcast_to(
        slope_blocks[:, None], (seq_count, batch_count, share, local_length)
    ).reshape(groups, share, local_length)
    slope_home = lax.all_to_all(slope_send, ("seq", "dp"), 0, 0, tiled=True)

    pair_home = pair_home.reshape(groups, 2, share, local_length)
    pair_home = jnp.transpose(pair_home, (1, 0, 2, 3)).reshape(2, chan_width, local_length)
    conv_rows = pair_home[0].T.astype(jnp.float32)
    corr_rows = pair_home[1].T.astype(jnp.float32)
    grad_filter = factor * slope_home.reshape(chan_width, local_length).T.astype(jnp.float32)

    signal = conv_rows + skip_gain[None, :] * mixed_wide
    output = (query_rows * signal).astype(jnp.bfloat16)
    grad_query = (cot_rows * signal).astype(jnp.bfloat16)
    back = corr_rows + skip_gain[None, :] * weighted_wide
    grad_key = (back * value_rows).astype(jnp.bfloat16)
    grad_value = (back * key_rows).astype(jnp.bfloat16)
    return (
        output[None],
        grad_query[None],
        grad_key[None],
        grad_value[None],
        grad_filter,
        grad_skip,
    )


def solution(mesh):
    return jax.shard_map(
        on_device,
        mesh=mesh,
        in_specs=(
            P("dp", "seq", "chan"),
            P("dp", "seq", "chan"),
            P("dp", "seq", "chan"),
            P("dp", "seq", "chan"),
            P("seq", "chan"),
            P("chan"),
        ),
        out_specs=(
            P("dp", "seq", "chan"),
            P("dp", "seq", "chan"),
            P("dp", "seq", "chan"),
            P("dp", "seq", "chan"),
            P("seq", "chan"),
            P("chan"),
        ),
        check_vma=False,
    )
```

```python
import math

import jax
import jax.numpy as jnp
from jax import lax
from jax.experimental import pallas as pl
from jax.experimental.pallas import tpu as pltpu
from jax.sharding import PartitionSpec as P

full_precision = lax.Precision.HIGHEST


def spectral_tables(seq_length):
    full_size = 2 * seq_length
    inner = 128
    outer = full_size // inner
    rows = seq_length // inner
    half = outer // 2 + 1
    k_index = jnp.arange(half, dtype=jnp.int32)
    n_index = jnp.arange(rows, dtype=jnp.int32)
    m_index = jnp.arange(inner, dtype=jnp.int32)
    j_index = jnp.arange(inner, dtype=jnp.int32)
    first_angle = (2.0 * math.pi / outer) * (
        (k_index[:, None] * n_index[None, :]) % outer
    ).astype(jnp.float32)
    first_cos = jnp.cos(first_angle)
    first_sin = jnp.sin(first_angle)
    stage_a = jnp.concatenate([first_cos, -first_sin], axis=0)
    weight = jnp.where((k_index == 0) | (k_index == outer // 2), 1.0, 2.0) / full_size
    inv_a = jnp.concatenate(
        [(first_cos * weight[:, None]).T, (-first_sin * weight[:, None]).T], axis=1
    )
    twist_angle = (2.0 * math.pi / full_size) * (
        (k_index[:, None] * m_index[None, :]) % full_size
    ).astype(jnp.float32)
    twist_cos, twist_sin = jnp.cos(twist_angle), jnp.sin(twist_angle)
    last_angle = (2.0 * math.pi / inner) * (
        (j_index[:, None] * m_index[None, :]) % inner
    ).astype(jnp.float32)
    last_cos, last_sin = jnp.cos(last_angle), jnp.sin(last_angle)
    g_re = twist_cos[:, None, :] * last_cos[None] - twist_sin[:, None, :] * last_sin[None]
    g_im = -(twist_sin[:, None, :] * last_cos[None] + twist_cos[:, None, :] * last_sin[None])
    fwd_table = jnp.concatenate([g_re, g_im], axis=1).astype(jnp.bfloat16)
    g_re_t = jnp.swapaxes(g_re, 1, 2)
    g_im_t = jnp.swapaxes(g_im, 1, 2)
    inv_table = jnp.concatenate([g_re_t, -g_im_t], axis=1).astype(jnp.bfloat16)
    return stage_a, inv_a, fwd_table, inv_table


def complex_stage(table, real_part, imag_part):
    inner = real_part.shape[1]
    a = jnp.einsum(
        "kjm,kml->kjl", table, real_part.astype(jnp.bfloat16),
        preferred_element_type=jnp.float32,
    )
    b = jnp.einsum(
        "kjm,kml->kjl", table, imag_part.astype(jnp.bfloat16),
        preferred_element_type=jnp.float32,
    )
    out_real = a[:, :inner] - b[:, inner:]
    out_imag = b[:, :inner] + a[:, inner:]
    return out_real, out_imag


def forward_spectrum(slab, tables):
    stage_a, _, fwd_table, _ = tables
    half = fwd_table.shape[0]
    first = jnp.einsum("kn,nml->kml", stage_a, slab, precision=full_precision)
    return complex_stage(fwd_table, first[:half], first[half:])


def inverse_spectrum(prod_re, prod_im, tables):
    _, inv_a, _, inv_table = tables
    back_re, back_im = complex_stage(inv_table, prod_re, prod_im)
    both = jnp.concatenate([back_re, back_im], axis=0)
    return jnp.einsum("nk,kml->nml", inv_a, both, precision=full_precision)


def middle_kernel(
    sig_re_ref, sig_im_ref, taps_re_ref, taps_im_ref, fwd_ref, inv_ref,
    pair_re_ref, pair_im_ref, cross_re_ref, cross_im_ref,
):
    steps, inner, lanes = sig_re_ref.shape
    half_lanes = lanes // 2
    lane = lax.broadcasted_iota(jnp.int32, (inner, lanes), 1)
    for step in range(steps):
        first = jnp.concatenate(
            [sig_re_ref[step], sig_im_ref[step], taps_re_ref[step], taps_im_ref[step]], axis=1
        ).astype(jnp.bfloat16)
        spec = jnp.dot(fwd_ref[step], first, preferred_element_type=jnp.float32)
        sig_re = spec[:inner, 0:lanes] - spec[inner:, lanes : 2 * lanes]
        sig_im = spec[:inner, lanes : 2 * lanes] + spec[inner:, 0:lanes]
        taps_re = spec[:inner, 2 * lanes : 3 * lanes] - spec[inner:, 3 * lanes :]
        taps_im = spec[:inner, 3 * lanes :] + spec[inner:, 2 * lanes : 3 * lanes]
        taps_im = jnp.where(lane < half_lanes, taps_im, -taps_im)
        pair_re = sig_re * taps_re - sig_im * taps_im
        pair_im = sig_re * taps_im + sig_im * taps_re
        turned_re = pltpu.roll(sig_re, half_lanes, 1)
        turned_im = pltpu.roll(sig_im, half_lanes, 1)
        cross_re = sig_re * turned_re + sig_im * turned_im
        cross_im = sig_re * turned_im - sig_im * turned_re
        second = jnp.concatenate([pair_re, pair_im, cross_re, cross_im], axis=1).astype(
            jnp.bfloat16
        )
        back = jnp.dot(inv_ref[step], second, preferred_element_type=jnp.float32)
        pair_re_ref[step] = back[:inner, 0:lanes] - back[inner:, lanes : 2 * lanes]
        pair_im_ref[step] = back[:inner, lanes : 2 * lanes] + back[inner:, 0:lanes]
        cross_re_ref[step] = back[:inner, 2 * lanes : 3 * lanes] - back[inner:, 3 * lanes :]
        cross_im_ref[step] = back[:inner, 3 * lanes :] + back[inner:, 2 * lanes : 3 * lanes]


def spectral_middle(sig_first, taps_first, fwd_table, inv_table):
    half, rows2, inner = fwd_table.shape
    lanes = sig_first.shape[2]
    steps = 3 if half % 3 == 0 else 1
    count = half // steps
    block = pl.BlockSpec((steps, inner, lanes), lambda k: (k, 0, 0))
    block_im = pl.BlockSpec((steps, inner, lanes), lambda k: (k + count, 0, 0))
    table_block = pl.BlockSpec((steps, rows2, inner), lambda k: (k, 0, 0))
    out_shape = jax.ShapeDtypeStruct((half, inner, lanes), jnp.float32)
    flops = half * 2 * 2 * rows2 * inner * 4 * lanes
    bytes_accessed = half * (8 * inner * lanes * 4 + 2 * rows2 * inner * 2)
    return pl.pallas_call(
        middle_kernel,
        grid=(count,),
        in_specs=[block, block_im, block, block_im, table_block, table_block],
        out_specs=[block] * 4,
        out_shape=[out_shape] * 4,
        cost_estimate=pl.CostEstimate(
            flops=flops, transcendentals=0, bytes_accessed=bytes_accessed
        ),
    )(sig_first, sig_first, taps_first, taps_first, fwd_table, inv_table)


def spectral_products(signals, taps, carry):
    seq_length, lanes = signals.shape
    tables = spectral_tables(seq_length)
    stage_a, _, fwd_table, inv_table = tables
    inner = fwd_table.shape[2]
    rows = seq_length // inner
    taps_first = jnp.einsum(
        "kn,nml->kml", stage_a, taps.reshape(rows, inner, lanes), precision=full_precision
    )
    sig_first = jnp.einsum(
        "kn,nml->kml", stage_a, signals.reshape(rows, inner, lanes), precision=full_precision
    )
    pair_re, pair_im, cross_re, cross_im = spectral_middle(
        sig_first, taps_first, fwd_table, inv_table
    )
    carry, pair_re, pair_im, cross_re, cross_im = lax.optimization_barrier(
        (carry, pair_re, pair_im, cross_re, cross_im)
    )
    return tables, (pair_re, pair_im), (cross_re, cross_im), carry


def spectral_inverse(back_re, back_im, tables):
    inv_a = tables[1]
    both = jnp.concatenate([back_re, back_im], axis=0)
    return jnp.einsum("nk,kml->nml", inv_a, both, precision=full_precision)


def on_device(query_proj, key_proj, value_proj, cotangent, long_filter, skip_gain):
    query_rows = query_proj[0].astype(jnp.float32)
    key_rows = key_proj[0].astype(jnp.float32)
    value_rows = value_proj[0].astype(jnp.float32)
    cot_rows = cotangent[0].astype(jnp.float32)
    local_length, chan_width = query_proj.shape[1], query_proj.shape[2]
    seq_count = lax.axis_size("seq")
    batch_count = lax.axis_size("dp")
    groups = seq_count * batch_count
    share = chan_width // groups
    seq_length = seq_count * local_length
    factor = (batch_count * seq_length) ** (-0.5)
    mixed = (key_rows * value_rows).astype(jnp.bfloat16)
    weighted = (cot_rows * query_rows).astype(jnp.bfloat16)

    mixed_wide = mixed.astype(jnp.float32)
    weighted_wide = weighted.astype(jnp.float32)
    gain_part = jnp.sum(weighted_wide * mixed_wide, axis=0)

    pair = jnp.stack([mixed.T, weighted.T], axis=0).reshape(2, groups, share, local_length)
    pair = jnp.transpose(pair, (1, 0, 2, 3)).reshape(groups, 2 * share, local_length)
    half_length = local_length // batch_count
    taps_t = long_filter.T.reshape(groups, share, batch_count, half_length)
    taps_mine = lax.dynamic_index_in_dim(taps_t, lax.axis_index("dp"), axis=2, keepdims=False)
    taps_rows = share * half_length // local_length
    taps_mine = taps_mine.astype(jnp.bfloat16).reshape(groups, taps_rows, local_length)
    taps_got = lax.all_to_all(taps_mine, ("seq", "dp"), 0, 0, tiled=True)
    taps_got, pair = lax.optimization_barrier((taps_got, pair))
    got = lax.all_to_all(pair, ("seq", "dp"), 0, 0, tiled=True)
    gain_part, got = lax.optimization_barrier((gain_part, got))
    total = gain_part
    distance = 1
    while distance < groups:
        partners = [(i, i ^ distance) for i in range(groups)]
        total = total + lax.ppermute(total, ("seq", "dp"), partners)
        distance *= 2
    grad_skip = factor * total

    pair_t = got.reshape(seq_count, batch_count, 2, share, local_length)
    signals = jnp.transpose(pair_t, (0, 4, 2, 1, 3)).reshape(seq_length, 2 * batch_count * share)
    taps_t = taps_got.reshape(seq_count, batch_count, share, half_length)
    taps = jnp.transpose(taps_t, (0, 1, 3, 2)).reshape(seq_length, 1, share)
    taps = jnp.broadcast_to(taps, (seq_length, 2 * batch_count, share)).reshape(
        seq_length, 2 * batch_count * share
    )

    tables, pair_spec, cross_spec, grad_skip = spectral_products(
        signals.astype(jnp.float32), taps.astype(jnp.float32), grad_skip
    )
    pair_vals = spectral_inverse(pair_spec[0], pair_spec[1], tables)
    pair_vals = pair_vals.reshape(seq_length, 2, batch_count, share)

    pair_back = pair_vals.astype(jnp.bfloat16).reshape(
        seq_count, local_length, 2, batch_count, share
    )
    pair_back = jnp.transpose(pair_back, (0, 3, 2, 4, 1)).reshape(
        groups, 2 * share, local_length
    )
    pair_home = lax.all_to_all(pair_back, ("seq", "dp"), 0, 0, tiled=True)

    cross = spectral_inverse(cross_spec[0], cross_spec[1], tables)
    cross = cross.reshape(seq_length, 2, batch_count, share)
    slope = jnp.sum(cross[:, 0], axis=1)
    slope_blocks = jnp.swapaxes(slope.astype(jnp.bfloat16).reshape(seq_count, local_length, share), 1, 2)
    slope_send = jnp.broadcast_to(
        slope_blocks[:, None], (seq_count, batch_count, share, local_length)
    ).reshape(groups, share, local_length)
    pair_home, slope_send = lax.optimization_barrier((pair_home, slope_send))
    slope_home = lax.all_to_all(slope_send, ("seq", "dp"), 0, 0, tiled=True)

    pair_home = pair_home.reshape(groups, 2, share, local_length)
    pair_home = jnp.transpose(pair_home, (1, 0, 2, 3)).reshape(2, chan_width, local_length)
    conv_rows = pair_home[0].T.astype(jnp.float32)
    corr_rows = pair_home[1].T.astype(jnp.float32)
    grad_filter = factor * slope_home.reshape(chan_width, local_length).T.astype(jnp.float32)

    signal = conv_rows + skip_gain[None, :] * mixed_wide
    output = (query_rows * signal).astype(jnp.bfloat16)
    grad_query = (cot_rows * signal).astype(jnp.bfloat16)
    back = corr_rows + skip_gain[None, :] * weighted_wide
    grad_key = (back * value_rows).astype(jnp.bfloat16)
    grad_value = (back * key_rows).astype(jnp.bfloat16)
    return (
        output[None],
        grad_query[None],
        grad_key[None],
        grad_value[None],
        grad_filter,
        grad_skip,
    )


def solution(mesh):
    return jax.shard_map(
        on_device,
        mesh=mesh,
        in_specs=(
            P("dp", "seq", "chan"),
            P("dp", "seq", "chan"),
            P("dp", "seq", "chan"),
            P("dp", "seq", "chan"),
            P("seq", "chan"),
            P("chan"),
        ),
        out_specs=(
            P("dp", "seq", "chan"),
            P("dp", "seq", "chan"),
            P("dp", "seq", "chan"),
            P("dp", "seq", "chan"),
            P("seq", "chan"),
            P("chan"),
        ),
        check_vma=False,
    )
```

```python
import math

import jax
import jax.numpy as jnp
from jax import lax
from jax.experimental import pallas as pl
from jax.experimental.pallas import tpu as pltpu
from jax.sharding import PartitionSpec as P

full_precision = lax.Precision.HIGHEST


def spectral_tables(seq_length):
    full_size = 2 * seq_length
    inner = 128
    outer = full_size // inner
    rows = seq_length // inner
    half = outer // 2 + 1
    k_index = jnp.arange(half, dtype=jnp.int32)
    n_index = jnp.arange(rows, dtype=jnp.int32)
    m_index = jnp.arange(inner, dtype=jnp.int32)
    j_index = jnp.arange(inner, dtype=jnp.int32)
    first_angle = (2.0 * math.pi / outer) * (
        (k_index[:, None] * n_index[None, :]) % outer
    ).astype(jnp.float32)
    first_cos = jnp.cos(first_angle)
    first_sin = jnp.sin(first_angle)
    stage_a = jnp.concatenate([first_cos, -first_sin], axis=0)
    weight = jnp.where((k_index == 0) | (k_index == outer // 2), 1.0, 2.0) / full_size
    inv_a = jnp.concatenate(
        [(first_cos * weight[:, None]).T, (-first_sin * weight[:, None]).T], axis=1
    )
    twist_angle = (2.0 * math.pi / full_size) * (
        (k_index[:, None] * m_index[None, :]) % full_size
    ).astype(jnp.float32)
    twist_cos, twist_sin = jnp.cos(twist_angle), jnp.sin(twist_angle)
    last_angle = (2.0 * math.pi / inner) * (
        (j_index[:, None] * m_index[None, :]) % inner
    ).astype(jnp.float32)
    last_cos, last_sin = jnp.cos(last_angle), jnp.sin(last_angle)
    g_re = twist_cos[:, None, :] * last_cos[None] - twist_sin[:, None, :] * last_sin[None]
    g_im = -(twist_sin[:, None, :] * last_cos[None] + twist_cos[:, None, :] * last_sin[None])
    fwd_table = jnp.concatenate([g_re, g_im], axis=1).astype(jnp.bfloat16)
    g_re_t = jnp.swapaxes(g_re, 1, 2)
    g_im_t = jnp.swapaxes(g_im, 1, 2)
    inv_table = jnp.concatenate([g_re_t, -g_im_t], axis=1).astype(jnp.bfloat16)
    return stage_a, inv_a, fwd_table, inv_table


def complex_stage(table, real_part, imag_part):
    inner = real_part.shape[1]
    a = jnp.einsum(
        "kjm,kml->kjl", table, real_part.astype(jnp.bfloat16),
        preferred_element_type=jnp.float32,
    )
    b = jnp.einsum(
        "kjm,kml->kjl", table, imag_part.astype(jnp.bfloat16),
        preferred_element_type=jnp.float32,
    )
    out_real = a[:, :inner] - b[:, inner:]
    out_imag = b[:, :inner] + a[:, inner:]
    return out_real, out_imag


def forward_spectrum(slab, tables):
    stage_a, _, fwd_table, _ = tables
    half = fwd_table.shape[0]
    first = jnp.einsum("kn,nml->kml", stage_a, slab, precision=full_precision)
    return complex_stage(fwd_table, first[:half], first[half:])


def inverse_spectrum(prod_re, prod_im, tables):
    _, inv_a, _, inv_table = tables
    back_re, back_im = complex_stage(inv_table, prod_re, prod_im)
    both = jnp.concatenate([back_re, back_im], axis=0)
    return jnp.einsum("nk,kml->nml", inv_a, both, precision=full_precision)


def middle_kernel(
    sig_re_ref, sig_im_ref, taps_re_ref, taps_im_ref, fwd_ref, inv_ref,
    pair_re_ref, pair_im_ref, cross_re_ref, cross_im_ref,
):
    steps, inner, lanes = sig_re_ref.shape
    half_lanes = lanes // 2
    lane = lax.broadcasted_iota(jnp.int32, (inner, lanes), 1)
    for step in range(steps):
        first = jnp.concatenate(
            [sig_re_ref[step], sig_im_ref[step], taps_re_ref[step], taps_im_ref[step]], axis=1
        ).astype(jnp.bfloat16)
        spec = jnp.dot(fwd_ref[step], first, preferred_element_type=jnp.float32)
        sig_re = spec[:inner, 0:lanes] - spec[inner:, lanes : 2 * lanes]
        sig_im = spec[:inner, lanes : 2 * lanes] + spec[inner:, 0:lanes]
        taps_re = spec[:inner, 2 * lanes : 3 * lanes] - spec[inner:, 3 * lanes :]
        taps_im = spec[:inner, 3 * lanes :] + spec[inner:, 2 * lanes : 3 * lanes]
        taps_im = jnp.where(lane < half_lanes, taps_im, -taps_im)
        pair_re = sig_re * taps_re - sig_im * taps_im
        pair_im = sig_re * taps_im + sig_im * taps_re
        turned_re = pltpu.roll(sig_re, half_lanes, 1)
        turned_im = pltpu.roll(sig_im, half_lanes, 1)
        cross_re = sig_re * turned_re + sig_im * turned_im
        cross_im = sig_re * turned_im - sig_im * turned_re
        second = jnp.concatenate([pair_re, pair_im, cross_re, cross_im], axis=1).astype(
            jnp.bfloat16
        )
        back = jnp.dot(inv_ref[step], second, preferred_element_type=jnp.float32)
        pair_re_ref[step] = back[:inner, 0:lanes] - back[inner:, lanes : 2 * lanes]
        pair_im_ref[step] = back[:inner, lanes : 2 * lanes] + back[inner:, 0:lanes]
        cross_re_ref[step] = back[:inner, 2 * lanes : 3 * lanes] - back[inner:, 3 * lanes :]
        cross_im_ref[step] = back[:inner, 3 * lanes :] + back[inner:, 2 * lanes : 3 * lanes]


def spectral_middle(sig_first, taps_first, fwd_table, inv_table):
    half, rows2, inner = fwd_table.shape
    lanes = sig_first.shape[2]
    steps = 3 if half % 3 == 0 else 1
    count = half // steps
    block = pl.BlockSpec((steps, inner, lanes), lambda k: (k, 0, 0))
    block_im = pl.BlockSpec((steps, inner, lanes), lambda k: (k + count, 0, 0))
    table_block = pl.BlockSpec((steps, rows2, inner), lambda k: (k, 0, 0))
    out_shape = jax.ShapeDtypeStruct((half, inner, lanes), jnp.float32)
    flops = half * 2 * 2 * rows2 * inner * 4 * lanes
    bytes_accessed = half * (8 * inner * lanes * 4 + 2 * rows2 * inner * 2)
    return pl.pallas_call(
        middle_kernel,
        grid=(count,),
        in_specs=[block, block_im, block, block_im, table_block, table_block],
        out_specs=[block] * 4,
        out_shape=[out_shape] * 4,
        cost_estimate=pl.CostEstimate(
            flops=flops, transcendentals=0, bytes_accessed=bytes_accessed
        ),
    )(sig_first, sig_first, taps_first, taps_first, fwd_table, inv_table)


def taps_spectrum_first(taps):
    seq_length, lanes = taps.shape
    tables = spectral_tables(seq_length)
    stage_a, _, fwd_table, _ = tables
    inner = fwd_table.shape[2]
    rows = seq_length // inner
    taps_first = jnp.einsum(
        "kn,nml->kml", stage_a, taps.reshape(rows, inner, lanes), precision=full_precision
    )
    return tables, taps_first


def spectral_products(signals, taps_first, tables, carry):
    seq_length, lanes = signals.shape
    stage_a, _, fwd_table, inv_table = tables
    inner = fwd_table.shape[2]
    rows = seq_length // inner
    sig_first = jnp.einsum(
        "kn,nml->kml", stage_a, signals.reshape(rows, inner, lanes), precision=full_precision
    )
    pair_re, pair_im, cross_re, cross_im = spectral_middle(
        sig_first, taps_first, fwd_table, inv_table
    )
    carry, pair_re, pair_im, cross_re, cross_im = lax.optimization_barrier(
        (carry, pair_re, pair_im, cross_re, cross_im)
    )
    return tables, (pair_re, pair_im), (cross_re, cross_im), carry


def spectral_inverse(back_re, back_im, tables):
    inv_a = tables[1]
    both = jnp.concatenate([back_re, back_im], axis=0)
    return jnp.einsum("nk,kml->nml", inv_a, both, precision=full_precision)


def on_device(query_proj, key_proj, value_proj, cotangent, long_filter, skip_gain):
    query_rows = query_proj[0].astype(jnp.float32)
    key_rows = key_proj[0].astype(jnp.float32)
    value_rows = value_proj[0].astype(jnp.float32)
    cot_rows = cotangent[0].astype(jnp.float32)
    local_length, chan_width = query_proj.shape[1], query_proj.shape[2]
    seq_count = lax.axis_size("seq")
    batch_count = lax.axis_size("dp")
    groups = seq_count * batch_count
    share = chan_width // groups
    seq_length = seq_count * local_length
    factor = (batch_count * seq_length) ** (-0.5)
    mixed = (key_rows * value_rows).astype(jnp.bfloat16)
    weighted = (cot_rows * query_rows).astype(jnp.bfloat16)

    mixed_wide = mixed.astype(jnp.float32)
    weighted_wide = weighted.astype(jnp.float32)
    gain_part = jnp.sum(weighted_wide * mixed_wide, axis=0)

    pair = jnp.stack([mixed.T, weighted.T], axis=0).reshape(2, groups, share, local_length)
    pair = jnp.transpose(pair, (1, 0, 2, 3)).reshape(groups, 2 * share, local_length)
    half_length = local_length // batch_count
    taps_t = long_filter.T.reshape(groups, share, batch_count, half_length)
    taps_mine = lax.dynamic_index_in_dim(taps_t, lax.axis_index("dp"), axis=2, keepdims=False)
    taps_rows = share * half_length // local_length
    taps_mine = taps_mine.astype(jnp.bfloat16).reshape(groups, taps_rows, local_length)
    taps_got = lax.all_to_all(taps_mine, ("seq", "dp"), 0, 0, tiled=True)
    taps_got, pair = lax.optimization_barrier((taps_got, pair))
    got = lax.all_to_all(pair, ("seq", "dp"), 0, 0, tiled=True)
    taps_t = taps_got.reshape(seq_count, batch_count, share, half_length)
    taps = jnp.transpose(taps_t, (0, 1, 3, 2)).reshape(seq_length, 1, share)
    taps = jnp.broadcast_to(taps, (seq_length, 2 * batch_count, share)).reshape(
        seq_length, 2 * batch_count * share
    )
    tables, taps_first = taps_spectrum_first(taps.astype(jnp.float32))
    gain_part, got, tables, taps_first = lax.optimization_barrier(
        (gain_part, got, tables, taps_first)
    )
    total = gain_part
    distance = 1
    while distance < groups:
        partners = [(i, i ^ distance) for i in range(groups)]
        total = total + lax.ppermute(total, ("seq", "dp"), partners)
        distance *= 2
    grad_skip = factor * total

    pair_t = got.reshape(seq_count, batch_count, 2, share, local_length)
    signals = jnp.transpose(pair_t, (0, 4, 2, 1, 3)).reshape(seq_length, 2 * batch_count * share)

    tables, pair_spec, cross_spec, grad_skip = spectral_products(
        signals.astype(jnp.float32), taps_first, tables, grad_skip
    )
    pair_vals = spectral_inverse(pair_spec[0], pair_spec[1], tables)
    pair_vals = pair_vals.reshape(seq_length, 2, batch_count, share)

    pair_back = pair_vals.astype(jnp.bfloat16).reshape(
        seq_count, local_length, 2, batch_count, share
    )
    pair_back = jnp.transpose(pair_back, (0, 3, 2, 4, 1)).reshape(
        groups, 2 * share, local_length
    )
    pair_home = lax.all_to_all(pair_back, ("seq", "dp"), 0, 0, tiled=True)

    cross = spectral_inverse(cross_spec[0], cross_spec[1], tables)
    cross = cross.reshape(seq_length, 2, batch_count, share)
    slope = jnp.sum(cross[:, 0], axis=1)
    slope_blocks = jnp.swapaxes(slope.astype(jnp.bfloat16).reshape(seq_count, local_length, share), 1, 2)
    slope_send = jnp.broadcast_to(
        slope_blocks[:, None], (seq_count, batch_count, share, local_length)
    ).reshape(groups, share, local_length)
    pair_home, slope_send = lax.optimization_barrier((pair_home, slope_send))
    slope_home = lax.all_to_all(slope_send, ("seq", "dp"), 0, 0, tiled=True)

    pair_home = pair_home.reshape(groups, 2, share, local_length)
    pair_home = jnp.transpose(pair_home, (1, 0, 2, 3)).reshape(2, chan_width, local_length)
    conv_rows = pair_home[0].T.astype(jnp.float32)
    corr_rows = pair_home[1].T.astype(jnp.float32)
    grad_filter = factor * slope_home.reshape(chan_width, local_length).T.astype(jnp.float32)

    signal = conv_rows + skip_gain[None, :] * mixed_wide
    output = (query_rows * signal).astype(jnp.bfloat16)
    grad_query = (cot_rows * signal).astype(jnp.bfloat16)
    back = corr_rows + skip_gain[None, :] * weighted_wide
    grad_key = (back * value_rows).astype(jnp.bfloat16)
    grad_value = (back * key_rows).astype(jnp.bfloat16)
    return (
        output[None],
        grad_query[None],
        grad_key[None],
        grad_value[None],
        grad_filter,
        grad_skip,
    )


def solution(mesh):
    return jax.shard_map(
        on_device,
        mesh=mesh,
        in_specs=(
            P("dp", "seq", "chan"),
            P("dp", "seq", "chan"),
            P("dp", "seq", "chan"),
            P("dp", "seq", "chan"),
            P("seq", "chan"),
            P("chan"),
        ),
        out_specs=(
            P("dp", "seq", "chan"),
            P("dp", "seq", "chan"),
            P("dp", "seq", "chan"),
            P("dp", "seq", "chan"),
            P("seq", "chan"),
            P("chan"),
        ),
        check_vma=False,
    )
```

```python
import math

import jax
import jax.numpy as jnp
from jax import lax
from jax.experimental import pallas as pl
from jax.experimental.pallas import tpu as pltpu
from jax.sharding import PartitionSpec as P

full_precision = lax.Precision.HIGHEST


def spectral_tables(seq_length):
    full_size = 2 * seq_length
    inner = 128
    outer = full_size // inner
    rows = seq_length // inner
    half = outer // 2 + 1
    k_index = jnp.arange(half, dtype=jnp.int32)
    n_index = jnp.arange(rows, dtype=jnp.int32)
    m_index = jnp.arange(inner, dtype=jnp.int32)
    j_index = jnp.arange(inner, dtype=jnp.int32)
    first_angle = (2.0 * math.pi / outer) * (
        (k_index[:, None] * n_index[None, :]) % outer
    ).astype(jnp.float32)
    first_cos = jnp.cos(first_angle)
    first_sin = jnp.sin(first_angle)
    stage_a = jnp.concatenate([first_cos, -first_sin], axis=0)
    weight = jnp.where((k_index == 0) | (k_index == outer // 2), 1.0, 2.0) / full_size
    inv_a = jnp.concatenate(
        [(first_cos * weight[:, None]).T, (-first_sin * weight[:, None]).T], axis=1
    )
    twist_angle = (2.0 * math.pi / full_size) * (
        (k_index[:, None] * m_index[None, :]) % full_size
    ).astype(jnp.float32)
    twist_cos, twist_sin = jnp.cos(twist_angle), jnp.sin(twist_angle)
    last_angle = (2.0 * math.pi / inner) * (
        (j_index[:, None] * m_index[None, :]) % inner
    ).astype(jnp.float32)
    last_cos, last_sin = jnp.cos(last_angle), jnp.sin(last_angle)
    g_re = twist_cos[:, None, :] * last_cos[None] - twist_sin[:, None, :] * last_sin[None]
    g_im = -(twist_sin[:, None, :] * last_cos[None] + twist_cos[:, None, :] * last_sin[None])
    fwd_table = jnp.concatenate([g_re, g_im], axis=1).astype(jnp.bfloat16)
    g_re_t = jnp.swapaxes(g_re, 1, 2)
    g_im_t = jnp.swapaxes(g_im, 1, 2)
    inv_table = jnp.concatenate([g_re_t, -g_im_t], axis=1).astype(jnp.bfloat16)
    return stage_a, inv_a, fwd_table, inv_table


def complex_stage(table, real_part, imag_part):
    inner = real_part.shape[1]
    a = jnp.einsum(
        "kjm,kml->kjl", table, real_part.astype(jnp.bfloat16),
        preferred_element_type=jnp.float32,
    )
    b = jnp.einsum(
        "kjm,kml->kjl", table, imag_part.astype(jnp.bfloat16),
        preferred_element_type=jnp.float32,
    )
    out_real = a[:, :inner] - b[:, inner:]
    out_imag = b[:, :inner] + a[:, inner:]
    return out_real, out_imag


def forward_spectrum(slab, tables):
    stage_a, _, fwd_table, _ = tables
    half = fwd_table.shape[0]
    first = jnp.einsum("kn,nml->kml", stage_a, slab, precision=full_precision)
    return complex_stage(fwd_table, first[:half], first[half:])


def inverse_spectrum(prod_re, prod_im, tables):
    _, inv_a, _, inv_table = tables
    back_re, back_im = complex_stage(inv_table, prod_re, prod_im)
    both = jnp.concatenate([back_re, back_im], axis=0)
    return jnp.einsum("nk,kml->nml", inv_a, both, precision=full_precision)


def middle_kernel(
    sig_re_ref, sig_im_ref, taps_re_ref, taps_im_ref, fwd_ref, inv_ref,
    pair_ref, cross_ref,
):
    steps, inner, lanes = sig_re_ref.shape
    half_lanes = lanes // 2
    lane = lax.broadcasted_iota(jnp.int32, (inner, lanes), 1)
    for step in range(steps):
        first = jnp.concatenate(
            [sig_re_ref[step], sig_im_ref[step], taps_re_ref[step], taps_im_ref[step]], axis=1
        ).astype(jnp.bfloat16)
        spec = jnp.dot(fwd_ref[step], first, preferred_element_type=jnp.float32)
        sig_re = spec[:inner, 0:lanes] - spec[inner:, lanes : 2 * lanes]
        sig_im = spec[:inner, lanes : 2 * lanes] + spec[inner:, 0:lanes]
        taps_re = spec[:inner, 2 * lanes : 3 * lanes] - spec[inner:, 3 * lanes :]
        taps_im = spec[:inner, 3 * lanes :] + spec[inner:, 2 * lanes : 3 * lanes]
        taps_im = jnp.where(lane < half_lanes, taps_im, -taps_im)
        pair_re = sig_re * taps_re - sig_im * taps_im
        pair_im = sig_re * taps_im + sig_im * taps_re
        turned_re = pltpu.roll(sig_re, half_lanes, 1)
        turned_im = pltpu.roll(sig_im, half_lanes, 1)
        cross_re = sig_re * turned_re + sig_im * turned_im
        cross_im = sig_re * turned_im - sig_im * turned_re
        second = jnp.concatenate([pair_re, pair_im, cross_re, cross_im], axis=1).astype(
            jnp.bfloat16
        )
        back = jnp.dot(inv_ref[step], second, preferred_element_type=jnp.float32)
        pair_ref[0, step] = back[:inner, 0:lanes] - back[inner:, lanes : 2 * lanes]
        pair_ref[1, step] = back[:inner, lanes : 2 * lanes] + back[inner:, 0:lanes]
        cross_ref[0, step] = back[:inner, 2 * lanes : 3 * lanes] - back[inner:, 3 * lanes :]
        cross_ref[1, step] = back[:inner, 3 * lanes :] + back[inner:, 2 * lanes : 3 * lanes]


def spectral_middle(sig_first, taps_first, fwd_table, inv_table):
    half, rows2, inner = fwd_table.shape
    lanes = sig_first.shape[2]
    steps = 3 if half % 3 == 0 else 1
    count = half // steps
    block = pl.BlockSpec((steps, inner, lanes), lambda k: (k, 0, 0))
    block_im = pl.BlockSpec((steps, inner, lanes), lambda k: (k + count, 0, 0))
    table_block = pl.BlockSpec((steps, rows2, inner), lambda k: (k, 0, 0))
    out_block = pl.BlockSpec((2, steps, inner, lanes), lambda k: (0, k, 0, 0))
    out_shape = jax.ShapeDtypeStruct((2, half, inner, lanes), jnp.float32)
    flops = half * 2 * 2 * rows2 * inner * 4 * lanes
    bytes_accessed = half * (4 * inner * lanes * 2 + 4 * inner * lanes * 4 + 2 * rows2 * inner * 2)
    return pl.pallas_call(
        middle_kernel,
        grid=(count,),
        in_specs=[block, block_im, block, block_im, table_block, table_block],
        out_specs=[out_block] * 2,
        out_shape=[out_shape] * 2,
        cost_estimate=pl.CostEstimate(
            flops=flops, transcendentals=0, bytes_accessed=bytes_accessed
        ),
    )(sig_first, sig_first, taps_first, taps_first, fwd_table, inv_table)


def taps_spectrum_first(taps):
    seq_length, lanes = taps.shape
    tables = spectral_tables(seq_length)
    stage_a, _, fwd_table, _ = tables
    inner = fwd_table.shape[2]
    rows = seq_length // inner
    taps_first = jnp.einsum(
        "kn,nml->kml", stage_a, taps.reshape(rows, inner, lanes), precision=full_precision
    )
    return tables, taps_first.astype(jnp.bfloat16)


def spectral_products(signals, taps_first, tables, carry):
    seq_length, lanes = signals.shape
    stage_a, _, fwd_table, inv_table = tables
    inner = fwd_table.shape[2]
    rows = seq_length // inner
    sig_first = jnp.einsum(
        "kn,nml->kml", stage_a, signals.reshape(rows, inner, lanes), precision=full_precision
    )
    pair_spec, cross_spec = spectral_middle(
        sig_first.astype(jnp.bfloat16), taps_first, fwd_table, inv_table
    )
    carry, pair_spec, cross_spec = lax.optimization_barrier((carry, pair_spec, cross_spec))
    return tables, pair_spec, cross_spec, carry


def spectral_inverse(back, tables):
    inv_a = tables[1]
    both = back.reshape((back.shape[0] * back.shape[1],) + back.shape[2:])
    return jnp.einsum("nk,kml->nml", inv_a, both, precision=full_precision)


def on_device(query_proj, key_proj, value_proj, cotangent, long_filter, skip_gain):
    query_rows = query_proj[0].astype(jnp.float32)
    key_rows = key_proj[0].astype(jnp.float32)
    value_rows = value_proj[0].astype(jnp.float32)
    cot_rows = cotangent[0].astype(jnp.float32)
    local_length, chan_width = query_proj.shape[1], query_proj.shape[2]
    seq_count = lax.axis_size("seq")
    batch_count = lax.axis_size("dp")
    groups = seq_count * batch_count
    share = chan_width // groups
    seq_length = seq_count * local_length
    factor = (batch_count * seq_length) ** (-0.5)
    mixed = (key_rows * value_rows).astype(jnp.bfloat16)
    weighted = (cot_rows * query_rows).astype(jnp.bfloat16)

    mixed_wide = mixed.astype(jnp.float32)
    weighted_wide = weighted.astype(jnp.float32)
    gain_part = jnp.sum(weighted_wide * mixed_wide, axis=0)

    pair = jnp.stack([mixed.T, weighted.T], axis=0).reshape(2, groups, share, local_length)
    pair = jnp.transpose(pair, (1, 0, 2, 3)).reshape(groups, 2 * share, local_length)
    half_length = local_length // batch_count
    taps_t = long_filter.T.reshape(groups, share, batch_count, half_length)
    taps_mine = lax.dynamic_index_in_dim(taps_t, lax.axis_index("dp"), axis=2, keepdims=False)
    taps_rows = share * half_length // local_length
    taps_mine = taps_mine.astype(jnp.bfloat16).reshape(groups, taps_rows, local_length)
    taps_got = lax.all_to_all(taps_mine, ("seq", "dp"), 0, 0, tiled=True)
    taps_got, pair = lax.optimization_barrier((taps_got, pair))
    got = lax.all_to_all(pair, ("seq", "dp"), 0, 0, tiled=True)
    taps_t = taps_got.reshape(seq_count, batch_count, share, half_length)
    taps = jnp.transpose(taps_t, (0, 1, 3, 2)).reshape(seq_length, 1, share)
    taps = jnp.broadcast_to(taps, (seq_length, 2 * batch_count, share)).reshape(
        seq_length, 2 * batch_count * share
    )
    tables, taps_first = taps_spectrum_first(taps.astype(jnp.float32))
    gain_part, got, tables, taps_first = lax.optimization_barrier(
        (gain_part, got, tables, taps_first)
    )
    total = gain_part
    distance = 1
    while distance < groups:
        partners = [(i, i ^ distance) for i in range(groups)]
        total = total + lax.ppermute(total, ("seq", "dp"), partners)
        distance *= 2
    grad_skip = factor * total

    pair_t = got.reshape(seq_count, batch_count, 2, share, local_length)
    signals = jnp.transpose(pair_t, (0, 4, 2, 1, 3)).reshape(seq_length, 2 * batch_count * share)

    tables, pair_spec, cross_spec, grad_skip = spectral_products(
        signals.astype(jnp.float32), taps_first, tables, grad_skip
    )
    pair_vals = spectral_inverse(pair_spec, tables)
    pair_vals = pair_vals.reshape(seq_length, 2, batch_count, share)

    pair_back = pair_vals.astype(jnp.bfloat16).reshape(
        seq_count, local_length, 2, batch_count, share
    )
    pair_back = jnp.transpose(pair_back, (0, 3, 2, 4, 1)).reshape(
        groups, 2 * share, local_length
    )
    pair_home = lax.all_to_all(pair_back, ("seq", "dp"), 0, 0, tiled=True)

    cross = spectral_inverse(cross_spec, tables)
    cross = cross.reshape(seq_length, 2, batch_count, share)
    slope = jnp.sum(cross[:, 0], axis=1)
    slope_blocks = jnp.swapaxes(slope.astype(jnp.bfloat16).reshape(seq_count, local_length, share), 1, 2)
    slope_send = jnp.broadcast_to(
        slope_blocks[:, None], (seq_count, batch_count, share, local_length)
    ).reshape(groups, share, local_length)
    pair_home, slope_send = lax.optimization_barrier((pair_home, slope_send))
    slope_home = lax.all_to_all(slope_send, ("seq", "dp"), 0, 0, tiled=True)

    pair_home = pair_home.reshape(groups, 2, share, local_length)
    pair_home = jnp.transpose(pair_home, (1, 0, 2, 3)).reshape(2, chan_width, local_length)
    conv_rows = pair_home[0].T.astype(jnp.float32)
    corr_rows = pair_home[1].T.astype(jnp.float32)
    grad_filter = factor * slope_home.reshape(chan_width, local_length).T.astype(jnp.float32)

    signal = conv_rows + skip_gain[None, :] * mixed_wide
    output = (query_rows * signal).astype(jnp.bfloat16)
    grad_query = (cot_rows * signal).astype(jnp.bfloat16)
    back = corr_rows + skip_gain[None, :] * weighted_wide
    grad_key = (back * value_rows).astype(jnp.bfloat16)
    grad_value = (back * key_rows).astype(jnp.bfloat16)
    return (
        output[None],
        grad_query[None],
        grad_key[None],
        grad_value[None],
        grad_filter,
        grad_skip,
    )


def solution(mesh):
    return jax.shard_map(
        on_device,
        mesh=mesh,
        in_specs=(
            P("dp", "seq", "chan"),
            P("dp", "seq", "chan"),
            P("dp", "seq", "chan"),
            P("dp", "seq", "chan"),
            P("seq", "chan"),
            P("chan"),
        ),
        out_specs=(
            P("dp", "seq", "chan"),
            P("dp", "seq", "chan"),
            P("dp", "seq", "chan"),
            P("dp", "seq", "chan"),
            P("seq", "chan"),
            P("chan"),
        ),
        check_vma=False,
    )
```

```python
import math

import jax
import jax.numpy as jnp
from jax import lax
from jax.experimental import pallas as pl
from jax.experimental.pallas import tpu as pltpu
from jax.sharding import PartitionSpec as P

full_precision = lax.Precision.HIGH


def spectral_tables(seq_length):
    full_size = 2 * seq_length
    inner = 128
    outer = full_size // inner
    rows = seq_length // inner
    half = outer // 2 + 1
    k_index = jnp.arange(half, dtype=jnp.int32)
    n_index = jnp.arange(rows, dtype=jnp.int32)
    m_index = jnp.arange(inner, dtype=jnp.int32)
    j_index = jnp.arange(inner, dtype=jnp.int32)
    first_angle = (2.0 * math.pi / outer) * (
        (k_index[:, None] * n_index[None, :]) % outer
    ).astype(jnp.float32)
    first_cos = jnp.cos(first_angle)
    first_sin = jnp.sin(first_angle)
    stage_a = jnp.concatenate([first_cos, -first_sin], axis=0)
    weight = jnp.where((k_index == 0) | (k_index == outer // 2), 1.0, 2.0) / full_size
    inv_a = jnp.concatenate(
        [(first_cos * weight[:, None]).T, (-first_sin * weight[:, None]).T], axis=1
    )
    twist_angle = (2.0 * math.pi / full_size) * (
        (k_index[:, None] * m_index[None, :]) % full_size
    ).astype(jnp.float32)
    twist_cos, twist_sin = jnp.cos(twist_angle), jnp.sin(twist_angle)
    last_angle = (2.0 * math.pi / inner) * (
        (j_index[:, None] * m_index[None, :]) % inner
    ).astype(jnp.float32)
    last_cos, last_sin = jnp.cos(last_angle), jnp.sin(last_angle)
    g_re = twist_cos[:, None, :] * last_cos[None] - twist_sin[:, None, :] * last_sin[None]
    g_im = -(twist_sin[:, None, :] * last_cos[None] + twist_cos[:, None, :] * last_sin[None])
    fwd_table = jnp.concatenate([g_re, g_im], axis=1).astype(jnp.bfloat16)
    g_re_t = jnp.swapaxes(g_re, 1, 2)
    g_im_t = jnp.swapaxes(g_im, 1, 2)
    inv_table = jnp.concatenate([g_re_t, -g_im_t], axis=1).astype(jnp.bfloat16)
    return stage_a, inv_a, fwd_table, inv_table


def complex_stage(table, real_part, imag_part):
    inner = real_part.shape[1]
    a = jnp.einsum(
        "kjm,kml->kjl", table, real_part.astype(jnp.bfloat16),
        preferred_element_type=jnp.float32,
    )
    b = jnp.einsum(
        "kjm,kml->kjl", table, imag_part.astype(jnp.bfloat16),
        preferred_element_type=jnp.float32,
    )
    out_real = a[:, :inner] - b[:, inner:]
    out_imag = b[:, :inner] + a[:, inner:]
    return out_real, out_imag


def forward_spectrum(slab, tables):
    stage_a, _, fwd_table, _ = tables
    half = fwd_table.shape[0]
    first = jnp.einsum("kn,nml->kml", stage_a, slab, precision=full_precision)
    return complex_stage(fwd_table, first[:half], first[half:])


def inverse_spectrum(prod_re, prod_im, tables):
    _, inv_a, _, inv_table = tables
    back_re, back_im = complex_stage(inv_table, prod_re, prod_im)
    both = jnp.concatenate([back_re, back_im], axis=0)
    return jnp.einsum("nk,kml->nml", inv_a, both, precision=full_precision)


def middle_kernel(
    sig_re_ref, sig_im_ref, taps_re_ref, taps_im_ref, fwd_ref, inv_ref,
    pair_ref, cross_ref,
):
    steps, inner, lanes = sig_re_ref.shape
    half_lanes = lanes // 2
    lane = lax.broadcasted_iota(jnp.int32, (inner, lanes), 1)
    for step in range(steps):
        first = jnp.concatenate(
            [sig_re_ref[step], sig_im_ref[step], taps_re_ref[step], taps_im_ref[step]], axis=1
        ).astype(jnp.bfloat16)
        spec = jnp.dot(fwd_ref[step], first, preferred_element_type=jnp.float32)
        sig_re = spec[:inner, 0:lanes] - spec[inner:, lanes : 2 * lanes]
        sig_im = spec[:inner, lanes : 2 * lanes] + spec[inner:, 0:lanes]
        taps_re = spec[:inner, 2 * lanes : 3 * lanes] - spec[inner:, 3 * lanes :]
        taps_im = spec[:inner, 3 * lanes :] + spec[inner:, 2 * lanes : 3 * lanes]
        taps_im = jnp.where(lane < half_lanes, taps_im, -taps_im)
        pair_re = sig_re * taps_re - sig_im * taps_im
        pair_im = sig_re * taps_im + sig_im * taps_re
        turned_re = pltpu.roll(sig_re, half_lanes, 1)
        turned_im = pltpu.roll(sig_im, half_lanes, 1)
        cross_re = sig_re * turned_re + sig_im * turned_im
        cross_im = sig_re * turned_im - sig_im * turned_re
        second = jnp.concatenate([pair_re, pair_im, cross_re, cross_im], axis=1).astype(
            jnp.bfloat16
        )
        back = jnp.dot(inv_ref[step], second, preferred_element_type=jnp.float32)
        pair_ref[0, step] = back[:inner, 0:lanes] - back[inner:, lanes : 2 * lanes]
        pair_ref[1, step] = back[:inner, lanes : 2 * lanes] + back[inner:, 0:lanes]
        cross_ref[0, step] = back[:inner, 2 * lanes : 3 * lanes] - back[inner:, 3 * lanes :]
        cross_ref[1, step] = back[:inner, 3 * lanes :] + back[inner:, 2 * lanes : 3 * lanes]


def spectral_middle(sig_first, taps_first, fwd_table, inv_table):
    half, rows2, inner = fwd_table.shape
    lanes = sig_first.shape[2]
    steps = 3 if half % 3 == 0 else 1
    count = half // steps
    block = pl.BlockSpec((steps, inner, lanes), lambda k: (k, 0, 0))
    block_im = pl.BlockSpec((steps, inner, lanes), lambda k: (k + count, 0, 0))
    table_block = pl.BlockSpec((steps, rows2, inner), lambda k: (k, 0, 0))
    out_block = pl.BlockSpec((2, steps, inner, lanes), lambda k: (0, k, 0, 0))
    out_shape = jax.ShapeDtypeStruct((2, half, inner, lanes), jnp.float32)
    flops = half * 2 * 2 * rows2 * inner * 4 * lanes
    bytes_accessed = half * (4 * inner * lanes * 2 + 4 * inner * lanes * 4 + 2 * rows2 * inner * 2)
    return pl.pallas_call(
        middle_kernel,
        grid=(count,),
        in_specs=[block, block_im, block, block_im, table_block, table_block],
        out_specs=[out_block] * 2,
        out_shape=[out_shape] * 2,
        cost_estimate=pl.CostEstimate(
            flops=flops, transcendentals=0, bytes_accessed=bytes_accessed
        ),
    )(sig_first, sig_first, taps_first, taps_first, fwd_table, inv_table)


def taps_spectrum_first(taps):
    seq_length, lanes = taps.shape
    tables = spectral_tables(seq_length)
    stage_a, _, fwd_table, _ = tables
    inner = fwd_table.shape[2]
    rows = seq_length // inner
    taps_first = jnp.einsum(
        "kn,nml->kml", stage_a, taps.reshape(rows, inner, lanes), precision=full_precision
    )
    return tables, taps_first.astype(jnp.bfloat16)


def spectral_products(signals, taps_first, tables, carry):
    seq_length, lanes = signals.shape
    stage_a, _, fwd_table, inv_table = tables
    inner = fwd_table.shape[2]
    rows = seq_length // inner
    sig_first = jnp.einsum(
        "kn,nml->kml", stage_a, signals.reshape(rows, inner, lanes), precision=full_precision
    )
    pair_spec, cross_spec = spectral_middle(
        sig_first.astype(jnp.bfloat16), taps_first, fwd_table, inv_table
    )
    carry, pair_spec, cross_spec = lax.optimization_barrier((carry, pair_spec, cross_spec))
    return tables, pair_spec, cross_spec, carry


def spectral_inverse(back, tables):
    inv_a = tables[1]
    both = back.reshape((back.shape[0] * back.shape[1],) + back.shape[2:])
    return jnp.einsum("nk,kml->nml", inv_a, both, precision=full_precision)


def on_device(query_proj, key_proj, value_proj, cotangent, long_filter, skip_gain):
    query_rows = query_proj[0].astype(jnp.float32)
    key_rows = key_proj[0].astype(jnp.float32)
    value_rows = value_proj[0].astype(jnp.float32)
    cot_rows = cotangent[0].astype(jnp.float32)
    local_length, chan_width = query_proj.shape[1], query_proj.shape[2]
    seq_count = lax.axis_size("seq")
    batch_count = lax.axis_size("dp")
    groups = seq_count * batch_count
    share = chan_width // groups
    seq_length = seq_count * local_length
    factor = (batch_count * seq_length) ** (-0.5)
    mixed = (key_rows * value_rows).astype(jnp.bfloat16)
    weighted = (cot_rows * query_rows).astype(jnp.bfloat16)

    mixed_wide = mixed.astype(jnp.float32)
    weighted_wide = weighted.astype(jnp.float32)
    gain_part = jnp.sum(weighted_wide * mixed_wide, axis=0)

    pair = jnp.stack([mixed.T, weighted.T], axis=0).reshape(2, groups, share, local_length)
    pair = jnp.transpose(pair, (1, 0, 2, 3)).reshape(groups, 2 * share, local_length)
    half_length = local_length // batch_count
    taps_t = long_filter.T.reshape(groups, share, batch_count, half_length)
    taps_mine = lax.dynamic_index_in_dim(taps_t, lax.axis_index("dp"), axis=2, keepdims=False)
    taps_rows = share * half_length // local_length
    taps_mine = taps_mine.astype(jnp.bfloat16).reshape(groups, taps_rows, local_length)
    taps_got = lax.all_to_all(taps_mine, ("seq", "dp"), 0, 0, tiled=True)
    taps_got, pair = lax.optimization_barrier((taps_got, pair))
    got = lax.all_to_all(pair, ("seq", "dp"), 0, 0, tiled=True)
    taps_t = taps_got.reshape(seq_count, batch_count, share, half_length)
    taps = jnp.transpose(taps_t, (0, 1, 3, 2)).reshape(seq_length, 1, share)
    taps = jnp.broadcast_to(taps, (seq_length, 2 * batch_count, share)).reshape(
        seq_length, 2 * batch_count * share
    )
    tables, taps_first = taps_spectrum_first(taps.astype(jnp.float32))
    gain_part, got, tables, taps_first = lax.optimization_barrier(
        (gain_part, got, tables, taps_first)
    )
    total = gain_part
    distance = 1
    while distance < groups:
        partners = [(i, i ^ distance) for i in range(groups)]
        total = total + lax.ppermute(total, ("seq", "dp"), partners)
        distance *= 2
    grad_skip = factor * total

    pair_t = got.reshape(seq_count, batch_count, 2, share, local_length)
    signals = jnp.transpose(pair_t, (0, 4, 2, 1, 3)).reshape(seq_length, 2 * batch_count * share)

    tables, pair_spec, cross_spec, grad_skip = spectral_products(
        signals.astype(jnp.float32), taps_first, tables, grad_skip
    )
    pair_vals = spectral_inverse(pair_spec, tables)
    pair_vals = pair_vals.reshape(seq_length, 2, batch_count, share)

    pair_back = pair_vals.astype(jnp.bfloat16).reshape(
        seq_count, local_length, 2, batch_count, share
    )
    pair_back = jnp.transpose(pair_back, (0, 3, 2, 4, 1)).reshape(
        groups, 2 * share, local_length
    )
    pair_home = lax.all_to_all(pair_back, ("seq", "dp"), 0, 0, tiled=True)

    cross = spectral_inverse(cross_spec, tables)
    cross = cross.reshape(seq_length, 2, batch_count, share)
    slope = jnp.sum(cross[:, 0], axis=1)
    slope_blocks = jnp.swapaxes(slope.astype(jnp.bfloat16).reshape(seq_count, local_length, share), 1, 2)
    slope_send = jnp.broadcast_to(
        slope_blocks[:, None], (seq_count, batch_count, share, local_length)
    ).reshape(groups, share, local_length)
    pair_home, slope_send = lax.optimization_barrier((pair_home, slope_send))
    slope_home = lax.all_to_all(slope_send, ("seq", "dp"), 0, 0, tiled=True)

    pair_home = pair_home.reshape(groups, 2, share, local_length)
    pair_home = jnp.transpose(pair_home, (1, 0, 2, 3)).reshape(2, chan_width, local_length)
    conv_rows = pair_home[0].T.astype(jnp.float32)
    corr_rows = pair_home[1].T.astype(jnp.float32)
    grad_filter = factor * slope_home.reshape(chan_width, local_length).T.astype(jnp.float32)

    signal = conv_rows + skip_gain[None, :] * mixed_wide
    output = (query_rows * signal).astype(jnp.bfloat16)
    grad_query = (cot_rows * signal).astype(jnp.bfloat16)
    back = corr_rows + skip_gain[None, :] * weighted_wide
    grad_key = (back * value_rows).astype(jnp.bfloat16)
    grad_value = (back * key_rows).astype(jnp.bfloat16)
    return (
        output[None],
        grad_query[None],
        grad_key[None],
        grad_value[None],
        grad_filter,
        grad_skip,
    )


def solution(mesh):
    return jax.shard_map(
        on_device,
        mesh=mesh,
        in_specs=(
            P("dp", "seq", "chan"),
            P("dp", "seq", "chan"),
            P("dp", "seq", "chan"),
            P("dp", "seq", "chan"),
            P("seq", "chan"),
            P("chan"),
        ),
        out_specs=(
            P("dp", "seq", "chan"),
            P("dp", "seq", "chan"),
            P("dp", "seq", "chan"),
            P("dp", "seq", "chan"),
            P("seq", "chan"),
            P("chan"),
        ),
        check_vma=False,
    )
```

```python
import math

import jax
import jax.numpy as jnp
from jax import lax
from jax.experimental import pallas as pl
from jax.experimental.pallas import tpu as pltpu
from jax.sharding import PartitionSpec as P

full_precision = lax.Precision.DEFAULT


def spectral_tables(seq_length):
    full_size = 2 * seq_length
    inner = 128
    outer = full_size // inner
    rows = seq_length // inner
    half = outer // 2 + 1
    k_index = jnp.arange(half, dtype=jnp.int32)
    n_index = jnp.arange(rows, dtype=jnp.int32)
    m_index = jnp.arange(inner, dtype=jnp.int32)
    j_index = jnp.arange(inner, dtype=jnp.int32)
    first_angle = (2.0 * math.pi / outer) * (
        (k_index[:, None] * n_index[None, :]) % outer
    ).astype(jnp.float32)
    first_cos = jnp.cos(first_angle)
    first_sin = jnp.sin(first_angle)
    stage_a = jnp.concatenate([first_cos, -first_sin], axis=0)
    weight = jnp.where((k_index == 0) | (k_index == outer // 2), 1.0, 2.0) / full_size
    inv_a = jnp.concatenate(
        [(first_cos * weight[:, None]).T, (-first_sin * weight[:, None]).T], axis=1
    )
    twist_angle = (2.0 * math.pi / full_size) * (
        (k_index[:, None] * m_index[None, :]) % full_size
    ).astype(jnp.float32)
    twist_cos, twist_sin = jnp.cos(twist_angle), jnp.sin(twist_angle)
    last_angle = (2.0 * math.pi / inner) * (
        (j_index[:, None] * m_index[None, :]) % inner
    ).astype(jnp.float32)
    last_cos, last_sin = jnp.cos(last_angle), jnp.sin(last_angle)
    g_re = twist_cos[:, None, :] * last_cos[None] - twist_sin[:, None, :] * last_sin[None]
    g_im = -(twist_sin[:, None, :] * last_cos[None] + twist_cos[:, None, :] * last_sin[None])
    fwd_table = jnp.concatenate([g_re, g_im], axis=1).astype(jnp.bfloat16)
    g_re_t = jnp.swapaxes(g_re, 1, 2)
    g_im_t = jnp.swapaxes(g_im, 1, 2)
    inv_table = jnp.concatenate([g_re_t, -g_im_t], axis=1).astype(jnp.bfloat16)
    return stage_a, inv_a, fwd_table, inv_table


def complex_stage(table, real_part, imag_part):
    inner = real_part.shape[1]
    a = jnp.einsum(
        "kjm,kml->kjl", table, real_part.astype(jnp.bfloat16),
        preferred_element_type=jnp.float32,
    )
    b = jnp.einsum(
        "kjm,kml->kjl", table, imag_part.astype(jnp.bfloat16),
        preferred_element_type=jnp.float32,
    )
    out_real = a[:, :inner] - b[:, inner:]
    out_imag = b[:, :inner] + a[:, inner:]
    return out_real, out_imag


def forward_spectrum(slab, tables):
    stage_a, _, fwd_table, _ = tables
    half = fwd_table.shape[0]
    first = jnp.einsum("kn,nml->kml", stage_a, slab, precision=full_precision)
    return complex_stage(fwd_table, first[:half], first[half:])


def inverse_spectrum(prod_re, prod_im, tables):
    _, inv_a, _, inv_table = tables
    back_re, back_im = complex_stage(inv_table, prod_re, prod_im)
    both = jnp.concatenate([back_re, back_im], axis=0)
    return jnp.einsum("nk,kml->nml", inv_a, both, precision=full_precision)


def middle_kernel(
    sig_re_ref, sig_im_ref, taps_re_ref, taps_im_ref, fwd_ref, inv_ref,
    pair_ref, cross_ref,
):
    steps, inner, lanes = sig_re_ref.shape
    half_lanes = lanes // 2
    lane = lax.broadcasted_iota(jnp.int32, (inner, lanes), 1)
    for step in range(steps):
        first = jnp.concatenate(
            [sig_re_ref[step], sig_im_ref[step], taps_re_ref[step], taps_im_ref[step]], axis=1
        ).astype(jnp.bfloat16)
        spec = jnp.dot(fwd_ref[step], first, preferred_element_type=jnp.float32)
        sig_re = spec[:inner, 0:lanes] - spec[inner:, lanes : 2 * lanes]
        sig_im = spec[:inner, lanes : 2 * lanes] + spec[inner:, 0:lanes]
        taps_re = spec[:inner, 2 * lanes : 3 * lanes] - spec[inner:, 3 * lanes :]
        taps_im = spec[:inner, 3 * lanes :] + spec[inner:, 2 * lanes : 3 * lanes]
        taps_im = jnp.where(lane < half_lanes, taps_im, -taps_im)
        pair_re = sig_re * taps_re - sig_im * taps_im
        pair_im = sig_re * taps_im + sig_im * taps_re
        turned_re = pltpu.roll(sig_re, half_lanes, 1)
        turned_im = pltpu.roll(sig_im, half_lanes, 1)
        cross_re = sig_re * turned_re + sig_im * turned_im
        cross_im = sig_re * turned_im - sig_im * turned_re
        second = jnp.concatenate([pair_re, pair_im, cross_re, cross_im], axis=1).astype(
            jnp.bfloat16
        )
        back = jnp.dot(inv_ref[step], second, preferred_element_type=jnp.float32)
        pair_ref[0, step] = back[:inner, 0:lanes] - back[inner:, lanes : 2 * lanes]
        pair_ref[1, step] = back[:inner, lanes : 2 * lanes] + back[inner:, 0:lanes]
        cross_ref[0, step] = back[:inner, 2 * lanes : 3 * lanes] - back[inner:, 3 * lanes :]
        cross_ref[1, step] = back[:inner, 3 * lanes :] + back[inner:, 2 * lanes : 3 * lanes]


def spectral_middle(sig_first, taps_first, fwd_table, inv_table):
    half, rows2, inner = fwd_table.shape
    lanes = sig_first.shape[2]
    steps = 3 if half % 3 == 0 else 1
    count = half // steps
    block = pl.BlockSpec((steps, inner, lanes), lambda k: (k, 0, 0))
    block_im = pl.BlockSpec((steps, inner, lanes), lambda k: (k + count, 0, 0))
    table_block = pl.BlockSpec((steps, rows2, inner), lambda k: (k, 0, 0))
    out_block = pl.BlockSpec((2, steps, inner, lanes), lambda k: (0, k, 0, 0))
    out_shape = jax.ShapeDtypeStruct((2, half, inner, lanes), jnp.float32)
    flops = half * 2 * 2 * rows2 * inner * 4 * lanes
    bytes_accessed = half * (4 * inner * lanes * 2 + 4 * inner * lanes * 4 + 2 * rows2 * inner * 2)
    return pl.pallas_call(
        middle_kernel,
        grid=(count,),
        in_specs=[block, block_im, block, block_im, table_block, table_block],
        out_specs=[out_block] * 2,
        out_shape=[out_shape] * 2,
        cost_estimate=pl.CostEstimate(
            flops=flops, transcendentals=0, bytes_accessed=bytes_accessed
        ),
    )(sig_first, sig_first, taps_first, taps_first, fwd_table, inv_table)


def taps_spectrum_first(taps):
    seq_length, lanes = taps.shape
    tables = spectral_tables(seq_length)
    stage_a, _, fwd_table, _ = tables
    inner = fwd_table.shape[2]
    rows = seq_length // inner
    taps_first = jnp.einsum(
        "kn,nml->kml", stage_a, taps.reshape(rows, inner, lanes), precision=full_precision
    )
    return tables, taps_first.astype(jnp.bfloat16)


def spectral_products(signals, taps_first, tables, carry):
    seq_length, lanes = signals.shape
    stage_a, _, fwd_table, inv_table = tables
    inner = fwd_table.shape[2]
    rows = seq_length // inner
    sig_first = jnp.einsum(
        "kn,nml->kml", stage_a, signals.reshape(rows, inner, lanes), precision=full_precision
    )
    pair_spec, cross_spec = spectral_middle(
        sig_first.astype(jnp.bfloat16), taps_first, fwd_table, inv_table
    )
    carry, pair_spec, cross_spec = lax.optimization_barrier((carry, pair_spec, cross_spec))
    return tables, pair_spec, cross_spec, carry


def spectral_inverse(back, tables):
    inv_a = tables[1]
    both = back.reshape((back.shape[0] * back.shape[1],) + back.shape[2:])
    return jnp.einsum("nk,kml->nml", inv_a, both, precision=full_precision)


def on_device(query_proj, key_proj, value_proj, cotangent, long_filter, skip_gain):
    query_rows = query_proj[0].astype(jnp.float32)
    key_rows = key_proj[0].astype(jnp.float32)
    value_rows = value_proj[0].astype(jnp.float32)
    cot_rows = cotangent[0].astype(jnp.float32)
    local_length, chan_width = query_proj.shape[1], query_proj.shape[2]
    seq_count = lax.axis_size("seq")
    batch_count = lax.axis_size("dp")
    groups = seq_count * batch_count
    share = chan_width // groups
    seq_length = seq_count * local_length
    factor = (batch_count * seq_length) ** (-0.5)
    mixed = (key_rows * value_rows).astype(jnp.bfloat16)
    weighted = (cot_rows * query_rows).astype(jnp.bfloat16)

    mixed_wide = mixed.astype(jnp.float32)
    weighted_wide = weighted.astype(jnp.float32)
    gain_part = jnp.sum(weighted_wide * mixed_wide, axis=0)

    pair = jnp.stack([mixed.T, weighted.T], axis=0).reshape(2, groups, share, local_length)
    pair = jnp.transpose(pair, (1, 0, 2, 3)).reshape(groups, 2 * share, local_length)
    half_length = local_length // batch_count
    taps_t = long_filter.T.reshape(groups, share, batch_count, half_length)
    taps_mine = lax.dynamic_index_in_dim(taps_t, lax.axis_index("dp"), axis=2, keepdims=False)
    taps_rows = share * half_length // local_length
    taps_mine = taps_mine.astype(jnp.bfloat16).reshape(groups, taps_rows, local_length)
    taps_got = lax.all_to_all(taps_mine, ("seq", "dp"), 0, 0, tiled=True)
    taps_got, pair = lax.optimization_barrier((taps_got, pair))
    got = lax.all_to_all(pair, ("seq", "dp"), 0, 0, tiled=True)
    taps_t = taps_got.reshape(seq_count, batch_count, share, half_length)
    taps = jnp.transpose(taps_t, (0, 1, 3, 2)).reshape(seq_length, 1, share)
    taps = jnp.broadcast_to(taps, (seq_length, 2 * batch_count, share)).reshape(
        seq_length, 2 * batch_count * share
    )
    tables, taps_first = taps_spectrum_first(taps.astype(jnp.float32))
    gain_part, got, tables, taps_first = lax.optimization_barrier(
        (gain_part, got, tables, taps_first)
    )
    total = gain_part
    distance = 1
    while distance < groups:
        partners = [(i, i ^ distance) for i in range(groups)]
        total = total + lax.ppermute(total, ("seq", "dp"), partners)
        distance *= 2
    grad_skip = factor * total

    pair_t = got.reshape(seq_count, batch_count, 2, share, local_length)
    signals = jnp.transpose(pair_t, (0, 4, 2, 1, 3)).reshape(seq_length, 2 * batch_count * share)

    tables, pair_spec, cross_spec, grad_skip = spectral_products(
        signals.astype(jnp.float32), taps_first, tables, grad_skip
    )
    pair_vals = spectral_inverse(pair_spec, tables)
    pair_vals = pair_vals.reshape(seq_length, 2, batch_count, share)

    pair_back = pair_vals.astype(jnp.bfloat16).reshape(
        seq_count, local_length, 2, batch_count, share
    )
    pair_back = jnp.transpose(pair_back, (0, 3, 2, 4, 1)).reshape(
        groups, 2 * share, local_length
    )
    pair_home = lax.all_to_all(pair_back, ("seq", "dp"), 0, 0, tiled=True)

    cross = spectral_inverse(cross_spec, tables)
    cross = cross.reshape(seq_length, 2, batch_count, share)
    slope = jnp.sum(cross[:, 0], axis=1)
    slope_blocks = jnp.swapaxes(slope.astype(jnp.bfloat16).reshape(seq_count, local_length, share), 1, 2)
    slope_send = jnp.broadcast_to(
        slope_blocks[:, None], (seq_count, batch_count, share, local_length)
    ).reshape(groups, share, local_length)
    pair_home, slope_send = lax.optimization_barrier((pair_home, slope_send))
    slope_home = lax.all_to_all(slope_send, ("seq", "dp"), 0, 0, tiled=True)

    pair_home = pair_home.reshape(groups, 2, share, local_length)
    pair_home = jnp.transpose(pair_home, (1, 0, 2, 3)).reshape(2, chan_width, local_length)
    conv_rows = pair_home[0].T.astype(jnp.float32)
    corr_rows = pair_home[1].T.astype(jnp.float32)
    grad_filter = factor * slope_home.reshape(chan_width, local_length).T.astype(jnp.float32)

    signal = conv_rows + skip_gain[None, :] * mixed_wide
    output = (query_rows * signal).astype(jnp.bfloat16)
    grad_query = (cot_rows * signal).astype(jnp.bfloat16)
    back = corr_rows + skip_gain[None, :] * weighted_wide
    grad_key = (back * value_rows).astype(jnp.bfloat16)
    grad_value = (back * key_rows).astype(jnp.bfloat16)
    return (
        output[None],
        grad_query[None],
        grad_key[None],
        grad_value[None],
        grad_filter,
        grad_skip,
    )


def solution(mesh):
    return jax.shard_map(
        on_device,
        mesh=mesh,
        in_specs=(
            P("dp", "seq", "chan"),
            P("dp", "seq", "chan"),
            P("dp", "seq", "chan"),
            P("dp", "seq", "chan"),
            P("seq", "chan"),
            P("chan"),
        ),
        out_specs=(
            P("dp", "seq", "chan"),
            P("dp", "seq", "chan"),
            P("dp", "seq", "chan"),
            P("dp", "seq", "chan"),
            P("seq", "chan"),
            P("chan"),
        ),
        check_vma=False,
    )
```

```python
import math

import jax
import jax.numpy as jnp
from jax import lax
from jax.experimental import pallas as pl
from jax.experimental.pallas import tpu as pltpu
from jax.sharding import PartitionSpec as P

full_precision = lax.Precision.DEFAULT


def spectral_tables(seq_length):
    full_size = 2 * seq_length
    inner = 128
    outer = full_size // inner
    rows = seq_length // inner
    half = outer // 2 + 1
    k_index = jnp.arange(half, dtype=jnp.int32)
    n_index = jnp.arange(rows, dtype=jnp.int32)
    m_index = jnp.arange(inner, dtype=jnp.int32)
    j_index = jnp.arange(inner, dtype=jnp.int32)
    first_angle = (2.0 * math.pi / outer) * (
        (k_index[:, None] * n_index[None, :]) % outer
    ).astype(jnp.float32)
    first_cos = jnp.cos(first_angle)
    first_sin = jnp.sin(first_angle)
    stage_a = jnp.concatenate([first_cos, -first_sin], axis=0)
    weight = jnp.where((k_index == 0) | (k_index == outer // 2), 1.0, 2.0) / full_size
    inv_a = jnp.concatenate(
        [(first_cos * weight[:, None]).T, (-first_sin * weight[:, None]).T], axis=1
    )
    twist_angle = (2.0 * math.pi / full_size) * (
        (k_index[:, None] * m_index[None, :]) % full_size
    ).astype(jnp.float32)
    twist_cos, twist_sin = jnp.cos(twist_angle), jnp.sin(twist_angle)
    last_angle = (2.0 * math.pi / inner) * (
        (j_index[:, None] * m_index[None, :]) % inner
    ).astype(jnp.float32)
    last_cos, last_sin = jnp.cos(last_angle), jnp.sin(last_angle)
    g_re = twist_cos[:, None, :] * last_cos[None] - twist_sin[:, None, :] * last_sin[None]
    g_im = -(twist_sin[:, None, :] * last_cos[None] + twist_cos[:, None, :] * last_sin[None])
    fwd_table = jnp.concatenate([g_re, g_im], axis=1).astype(jnp.bfloat16)
    g_re_t = jnp.swapaxes(g_re, 1, 2)
    g_im_t = jnp.swapaxes(g_im, 1, 2)
    inv_table = jnp.concatenate([g_re_t, -g_im_t], axis=1).astype(jnp.bfloat16)
    return stage_a, inv_a, fwd_table, inv_table


def complex_stage(table, real_part, imag_part):
    inner = real_part.shape[1]
    a = jnp.einsum(
        "kjm,kml->kjl", table, real_part.astype(jnp.bfloat16),
        preferred_element_type=jnp.float32,
    )
    b = jnp.einsum(
        "kjm,kml->kjl", table, imag_part.astype(jnp.bfloat16),
        preferred_element_type=jnp.float32,
    )
    out_real = a[:, :inner] - b[:, inner:]
    out_imag = b[:, :inner] + a[:, inner:]
    return out_real, out_imag


def forward_spectrum(slab, tables):
    stage_a, _, fwd_table, _ = tables
    half = fwd_table.shape[0]
    first = jnp.einsum("kn,nml->kml", stage_a, slab, precision=full_precision)
    return complex_stage(fwd_table, first[:half], first[half:])


def inverse_spectrum(prod_re, prod_im, tables):
    _, inv_a, _, inv_table = tables
    back_re, back_im = complex_stage(inv_table, prod_re, prod_im)
    both = jnp.concatenate([back_re, back_im], axis=0)
    return jnp.einsum("nk,kml->nml", inv_a, both, precision=full_precision)


def middle_kernel(
    sig_re_ref, sig_im_ref, taps_re_ref, taps_im_ref, fwd_ref, inv_ref,
    pair_ref, cross_ref,
):
    steps, inner, lanes = sig_re_ref.shape
    half_lanes = lanes // 2
    lane = lax.broadcasted_iota(jnp.int32, (inner, lanes), 1)
    for step in range(steps):
        first = jnp.concatenate(
            [sig_re_ref[step], sig_im_ref[step], taps_re_ref[step], taps_im_ref[step]], axis=1
        ).astype(jnp.bfloat16)
        spec = jnp.dot(fwd_ref[step], first, preferred_element_type=jnp.float32)
        sig_re = spec[:inner, 0:lanes] - spec[inner:, lanes : 2 * lanes]
        sig_im = spec[:inner, lanes : 2 * lanes] + spec[inner:, 0:lanes]
        taps_re = spec[:inner, 2 * lanes : 3 * lanes] - spec[inner:, 3 * lanes :]
        taps_im = spec[:inner, 3 * lanes :] + spec[inner:, 2 * lanes : 3 * lanes]
        taps_im = jnp.where(lane < half_lanes, taps_im, -taps_im)
        pair_re = sig_re * taps_re - sig_im * taps_im
        pair_im = sig_re * taps_im + sig_im * taps_re
        turned_re = pltpu.roll(sig_re, half_lanes, 1)
        turned_im = pltpu.roll(sig_im, half_lanes, 1)
        cross_re = sig_re * turned_re + sig_im * turned_im
        cross_im = sig_re * turned_im - sig_im * turned_re
        second = jnp.concatenate([pair_re, pair_im, cross_re, cross_im], axis=1).astype(
            jnp.bfloat16
        )
        back = jnp.dot(inv_ref[step], second, preferred_element_type=jnp.float32)
        pair_ref[0, step] = back[:inner, 0:lanes] - back[inner:, lanes : 2 * lanes]
        pair_ref[1, step] = back[:inner, lanes : 2 * lanes] + back[inner:, 0:lanes]
        cross_ref[0, step] = back[:inner, 2 * lanes : 3 * lanes] - back[inner:, 3 * lanes :]
        cross_ref[1, step] = back[:inner, 3 * lanes :] + back[inner:, 2 * lanes : 3 * lanes]


def spectral_middle(sig_first, taps_first, fwd_table, inv_table):
    half, rows2, inner = fwd_table.shape
    lanes = sig_first.shape[2]
    steps = 11 if half % 11 == 0 else 1
    count = half // steps
    block = pl.BlockSpec((steps, inner, lanes), lambda k: (k, 0, 0))
    block_im = pl.BlockSpec((steps, inner, lanes), lambda k: (k + count, 0, 0))
    table_block = pl.BlockSpec((steps, rows2, inner), lambda k: (k, 0, 0))
    out_block = pl.BlockSpec((2, steps, inner, lanes), lambda k: (0, k, 0, 0))
    out_shape = jax.ShapeDtypeStruct((2, half, inner, lanes), jnp.float32)
    flops = half * 2 * 2 * rows2 * inner * 4 * lanes
    bytes_accessed = half * (4 * inner * lanes * 2 + 4 * inner * lanes * 4 + 2 * rows2 * inner * 2)
    return pl.pallas_call(
        middle_kernel,
        grid=(count,),
        in_specs=[block, block_im, block, block_im, table_block, table_block],
        out_specs=[out_block] * 2,
        out_shape=[out_shape] * 2,
        cost_estimate=pl.CostEstimate(
            flops=flops, transcendentals=0, bytes_accessed=bytes_accessed
        ),
    )(sig_first, sig_first, taps_first, taps_first, fwd_table, inv_table)


def taps_spectrum_first(taps):
    seq_length, lanes = taps.shape
    tables = spectral_tables(seq_length)
    stage_a, _, fwd_table, _ = tables
    inner = fwd_table.shape[2]
    rows = seq_length // inner
    taps_first = jnp.einsum(
        "kn,nml->kml", stage_a, taps.reshape(rows, inner, lanes), precision=full_precision
    )
    return tables, taps_first.astype(jnp.bfloat16)


def spectral_products(signals, taps_first, tables, carry):
    seq_length, lanes = signals.shape
    stage_a, _, fwd_table, inv_table = tables
    inner = fwd_table.shape[2]
    rows = seq_length // inner
    sig_first = jnp.einsum(
        "kn,nml->kml", stage_a, signals.reshape(rows, inner, lanes), precision=full_precision
    )
    pair_spec, cross_spec = spectral_middle(
        sig_first.astype(jnp.bfloat16), taps_first, fwd_table, inv_table
    )
    carry, pair_spec, cross_spec = lax.optimization_barrier((carry, pair_spec, cross_spec))
    return tables, pair_spec, cross_spec, carry


def spectral_inverse(back, tables):
    inv_a = tables[1]
    both = back.reshape((back.shape[0] * back.shape[1],) + back.shape[2:])
    return jnp.einsum("nk,kml->nml", inv_a, both, precision=full_precision)


def on_device(query_proj, key_proj, value_proj, cotangent, long_filter, skip_gain):
    query_rows = query_proj[0].astype(jnp.float32)
    key_rows = key_proj[0].astype(jnp.float32)
    value_rows = value_proj[0].astype(jnp.float32)
    cot_rows = cotangent[0].astype(jnp.float32)
    local_length, chan_width = query_proj.shape[1], query_proj.shape[2]
    seq_count = lax.axis_size("seq")
    batch_count = lax.axis_size("dp")
    groups = seq_count * batch_count
    share = chan_width // groups
    seq_length = seq_count * local_length
    factor = (batch_count * seq_length) ** (-0.5)
    mixed = (key_rows * value_rows).astype(jnp.bfloat16)
    weighted = (cot_rows * query_rows).astype(jnp.bfloat16)

    mixed_wide = mixed.astype(jnp.float32)
    weighted_wide = weighted.astype(jnp.float32)
    gain_part = jnp.sum(weighted_wide * mixed_wide, axis=0)

    pair = jnp.stack([mixed.T, weighted.T], axis=0).reshape(2, groups, share, local_length)
    pair = jnp.transpose(pair, (1, 0, 2, 3)).reshape(groups, 2 * share, local_length)
    half_length = local_length // batch_count
    taps_t = long_filter.T.reshape(groups, share, batch_count, half_length)
    taps_mine = lax.dynamic_index_in_dim(taps_t, lax.axis_index("dp"), axis=2, keepdims=False)
    taps_rows = share * half_length // local_length
    taps_mine = taps_mine.astype(jnp.bfloat16).reshape(groups, taps_rows, local_length)
    taps_got = lax.all_to_all(taps_mine, ("seq", "dp"), 0, 0, tiled=True)
    taps_got, pair = lax.optimization_barrier((taps_got, pair))
    got = lax.all_to_all(pair, ("seq", "dp"), 0, 0, tiled=True)
    taps_t = taps_got.reshape(seq_count, batch_count, share, half_length)
    taps = jnp.transpose(taps_t, (0, 1, 3, 2)).reshape(seq_length, 1, share)
    taps = jnp.broadcast_to(taps, (seq_length, 2 * batch_count, share)).reshape(
        seq_length, 2 * batch_count * share
    )
    tables, taps_first = taps_spectrum_first(taps.astype(jnp.float32))
    gain_part, got, tables, taps_first = lax.optimization_barrier(
        (gain_part, got, tables, taps_first)
    )
    total = gain_part
    distance = 1
    while distance < groups:
        partners = [(i, i ^ distance) for i in range(groups)]
        total = total + lax.ppermute(total, ("seq", "dp"), partners)
        distance *= 2
    grad_skip = factor * total

    pair_t = got.reshape(seq_count, batch_count, 2, share, local_length)
    signals = jnp.transpose(pair_t, (0, 4, 2, 1, 3)).reshape(seq_length, 2 * batch_count * share)

    tables, pair_spec, cross_spec, grad_skip = spectral_products(
        signals.astype(jnp.float32), taps_first, tables, grad_skip
    )
    pair_vals = spectral_inverse(pair_spec, tables)
    pair_vals = pair_vals.reshape(seq_length, 2, batch_count, share)

    pair_back = pair_vals.astype(jnp.bfloat16).reshape(
        seq_count, local_length, 2, batch_count, share
    )
    pair_back = jnp.transpose(pair_back, (0, 3, 2, 4, 1)).reshape(
        groups, 2 * share, local_length
    )
    pair_home = lax.all_to_all(pair_back, ("seq", "dp"), 0, 0, tiled=True)

    cross = spectral_inverse(cross_spec, tables)
    cross = cross.reshape(seq_length, 2, batch_count, share)
    slope = jnp.sum(cross[:, 0], axis=1)
    slope_blocks = jnp.swapaxes(slope.astype(jnp.bfloat16).reshape(seq_count, local_length, share), 1, 2)
    slope_send = jnp.broadcast_to(
        slope_blocks[:, None], (seq_count, batch_count, share, local_length)
    ).reshape(groups, share, local_length)
    pair_home, slope_send = lax.optimization_barrier((pair_home, slope_send))
    slope_home = lax.all_to_all(slope_send, ("seq", "dp"), 0, 0, tiled=True)

    pair_home = pair_home.reshape(groups, 2, share, local_length)
    pair_home = jnp.transpose(pair_home, (1, 0, 2, 3)).reshape(2, chan_width, local_length)
    conv_rows = pair_home[0].T.astype(jnp.float32)
    corr_rows = pair_home[1].T.astype(jnp.float32)
    grad_filter = factor * slope_home.reshape(chan_width, local_length).T.astype(jnp.float32)

    signal = conv_rows + skip_gain[None, :] * mixed_wide
    output = (query_rows * signal).astype(jnp.bfloat16)
    grad_query = (cot_rows * signal).astype(jnp.bfloat16)
    back = corr_rows + skip_gain[None, :] * weighted_wide
    grad_key = (back * value_rows).astype(jnp.bfloat16)
    grad_value = (back * key_rows).astype(jnp.bfloat16)
    return (
        output[None],
        grad_query[None],
        grad_key[None],
        grad_value[None],
        grad_filter,
        grad_skip,
    )


def solution(mesh):
    return jax.shard_map(
        on_device,
        mesh=mesh,
        in_specs=(
            P("dp", "seq", "chan"),
            P("dp", "seq", "chan"),
            P("dp", "seq", "chan"),
            P("dp", "seq", "chan"),
            P("seq", "chan"),
            P("chan"),
        ),
        out_specs=(
            P("dp", "seq", "chan"),
            P("dp", "seq", "chan"),
            P("dp", "seq", "chan"),
            P("dp", "seq", "chan"),
            P("seq", "chan"),
            P("chan"),
        ),
        check_vma=False,
    )
```

```python
import math

import jax
import jax.numpy as jnp
from jax import lax
from jax.experimental import pallas as pl
from jax.experimental.pallas import tpu as pltpu
from jax.sharding import PartitionSpec as P

full_precision = lax.Precision.DEFAULT


def spectral_tables(seq_length):
    full_size = 2 * seq_length
    inner = 128
    outer = full_size // inner
    rows = seq_length // inner
    half = outer // 2 + 1
    k_index = jnp.arange(half, dtype=jnp.int32)
    n_index = jnp.arange(rows, dtype=jnp.int32)
    m_index = jnp.arange(inner, dtype=jnp.int32)
    j_index = jnp.arange(inner, dtype=jnp.int32)
    first_angle = (2.0 * math.pi / outer) * (
        (k_index[:, None] * n_index[None, :]) % outer
    ).astype(jnp.float32)
    first_cos = jnp.cos(first_angle)
    first_sin = jnp.sin(first_angle)
    stage_a = jnp.concatenate([first_cos, -first_sin], axis=0)
    weight = jnp.where((k_index == 0) | (k_index == outer // 2), 1.0, 2.0) / full_size
    inv_a = jnp.concatenate(
        [(first_cos * weight[:, None]).T, (-first_sin * weight[:, None]).T], axis=1
    )
    twist_angle = (2.0 * math.pi / full_size) * (
        (k_index[:, None] * m_index[None, :]) % full_size
    ).astype(jnp.float32)
    twist_cos, twist_sin = jnp.cos(twist_angle), jnp.sin(twist_angle)
    last_angle = (2.0 * math.pi / inner) * (
        (j_index[:, None] * m_index[None, :]) % inner
    ).astype(jnp.float32)
    last_cos, last_sin = jnp.cos(last_angle), jnp.sin(last_angle)
    g_re = twist_cos[:, None, :] * last_cos[None] - twist_sin[:, None, :] * last_sin[None]
    g_im = -(twist_sin[:, None, :] * last_cos[None] + twist_cos[:, None, :] * last_sin[None])
    fwd_table = jnp.concatenate([g_re, g_im], axis=1).astype(jnp.bfloat16)
    g_re_t = jnp.swapaxes(g_re, 1, 2)
    g_im_t = jnp.swapaxes(g_im, 1, 2)
    inv_table = jnp.concatenate([g_re_t, -g_im_t], axis=1).astype(jnp.bfloat16)
    return stage_a, inv_a, fwd_table, inv_table


def complex_stage(table, real_part, imag_part):
    inner = real_part.shape[1]
    a = jnp.einsum(
        "kjm,kml->kjl", table, real_part.astype(jnp.bfloat16),
        preferred_element_type=jnp.float32,
    )
    b = jnp.einsum(
        "kjm,kml->kjl", table, imag_part.astype(jnp.bfloat16),
        preferred_element_type=jnp.float32,
    )
    out_real = a[:, :inner] - b[:, inner:]
    out_imag = b[:, :inner] + a[:, inner:]
    return out_real, out_imag


def forward_spectrum(slab, tables):
    stage_a, _, fwd_table, _ = tables
    half = fwd_table.shape[0]
    first = jnp.einsum("kn,nml->kml", stage_a, slab, precision=full_precision)
    return complex_stage(fwd_table, first[:half], first[half:])


def inverse_spectrum(prod_re, prod_im, tables):
    _, inv_a, _, inv_table = tables
    back_re, back_im = complex_stage(inv_table, prod_re, prod_im)
    both = jnp.concatenate([back_re, back_im], axis=0)
    return jnp.einsum("nk,kml->nml", inv_a, both, precision=full_precision)


def middle_kernel(
    sig_re_ref, sig_im_ref, taps_re_ref, taps_im_ref, fwd_ref, inv_ref,
    pair_ref, cross_ref,
):
    steps, inner, lanes = sig_re_ref.shape
    half_lanes = lanes // 2
    lane = lax.broadcasted_iota(jnp.int32, (inner, lanes), 1)
    for step in range(steps):
        first = jnp.concatenate(
            [sig_re_ref[step], sig_im_ref[step], taps_re_ref[step], taps_im_ref[step]], axis=1
        ).astype(jnp.bfloat16)
        spec = jnp.dot(fwd_ref[step], first, preferred_element_type=jnp.float32)
        sig_re = spec[:inner, 0:lanes] - spec[inner:, lanes : 2 * lanes]
        sig_im = spec[:inner, lanes : 2 * lanes] + spec[inner:, 0:lanes]
        taps_re = spec[:inner, 2 * lanes : 3 * lanes] - spec[inner:, 3 * lanes :]
        taps_im = spec[:inner, 3 * lanes :] + spec[inner:, 2 * lanes : 3 * lanes]
        taps_im = jnp.where(lane < half_lanes, taps_im, -taps_im)
        pair_re = sig_re * taps_re - sig_im * taps_im
        pair_im = sig_re * taps_im + sig_im * taps_re
        turned_re = pltpu.roll(sig_re, half_lanes, 1)
        turned_im = pltpu.roll(sig_im, half_lanes, 1)
        cross_re = sig_re * turned_re + sig_im * turned_im
        cross_im = sig_re * turned_im - sig_im * turned_re
        second = jnp.concatenate([pair_re, pair_im, cross_re, cross_im], axis=1).astype(
            jnp.bfloat16
        )
        back = jnp.dot(inv_ref[step], second, preferred_element_type=jnp.float32)
        pair_ref[0, step] = (back[:inner, 0:lanes] - back[inner:, lanes : 2 * lanes]).astype(pair_ref.dtype)
        pair_ref[1, step] = (back[:inner, lanes : 2 * lanes] + back[inner:, 0:lanes]).astype(pair_ref.dtype)
        cross_ref[0, step] = (back[:inner, 2 * lanes : 3 * lanes] - back[inner:, 3 * lanes :]).astype(cross_ref.dtype)
        cross_ref[1, step] = (back[:inner, 3 * lanes :] + back[inner:, 2 * lanes : 3 * lanes]).astype(cross_ref.dtype)


def spectral_middle(sig_first, taps_first, fwd_table, inv_table):
    half, rows2, inner = fwd_table.shape
    lanes = sig_first.shape[2]
    steps = 11 if half % 11 == 0 else 1
    count = half // steps
    block = pl.BlockSpec((steps, inner, lanes), lambda k: (k, 0, 0))
    block_im = pl.BlockSpec((steps, inner, lanes), lambda k: (k + count, 0, 0))
    table_block = pl.BlockSpec((steps, rows2, inner), lambda k: (k, 0, 0))
    out_block = pl.BlockSpec((2, steps, inner, lanes), lambda k: (0, k, 0, 0))
    out_shape = jax.ShapeDtypeStruct((2, half, inner, lanes), jnp.bfloat16)
    flops = half * 2 * 2 * rows2 * inner * 4 * lanes
    bytes_accessed = half * (4 * inner * lanes * 2 + 4 * inner * lanes * 4 + 2 * rows2 * inner * 2)
    return pl.pallas_call(
        middle_kernel,
        grid=(count,),
        in_specs=[block, block_im, block, block_im, table_block, table_block],
        out_specs=[out_block] * 2,
        out_shape=[out_shape] * 2,
        cost_estimate=pl.CostEstimate(
            flops=flops, transcendentals=0, bytes_accessed=bytes_accessed
        ),
    )(sig_first, sig_first, taps_first, taps_first, fwd_table, inv_table)


def taps_spectrum_first(taps):
    seq_length, lanes = taps.shape
    tables = spectral_tables(seq_length)
    stage_a, _, fwd_table, _ = tables
    inner = fwd_table.shape[2]
    rows = seq_length // inner
    taps_first = jnp.einsum(
        "kn,nml->kml", stage_a, taps.reshape(rows, inner, lanes), precision=full_precision
    )
    return tables, taps_first.astype(jnp.bfloat16)


def spectral_products(signals, taps_first, tables, carry):
    seq_length, lanes = signals.shape
    stage_a, _, fwd_table, inv_table = tables
    inner = fwd_table.shape[2]
    rows = seq_length // inner
    sig_first = jnp.einsum(
        "kn,nml->kml", stage_a, signals.reshape(rows, inner, lanes), precision=full_precision
    )
    pair_spec, cross_spec = spectral_middle(
        sig_first.astype(jnp.bfloat16), taps_first, fwd_table, inv_table
    )
    carry, pair_spec, cross_spec = lax.optimization_barrier((carry, pair_spec, cross_spec))
    return tables, pair_spec, cross_spec, carry


def spectral_inverse(back, tables):
    inv_a = tables[1]
    both = back.reshape((back.shape[0] * back.shape[1],) + back.shape[2:])
    return jnp.einsum("nk,kml->nml", inv_a, both, precision=full_precision)


def on_device(query_proj, key_proj, value_proj, cotangent, long_filter, skip_gain):
    query_rows = query_proj[0].astype(jnp.float32)
    key_rows = key_proj[0].astype(jnp.float32)
    value_rows = value_proj[0].astype(jnp.float32)
    cot_rows = cotangent[0].astype(jnp.float32)
    local_length, chan_width = query_proj.shape[1], query_proj.shape[2]
    seq_count = lax.axis_size("seq")
    batch_count = lax.axis_size("dp")
    groups = seq_count * batch_count
    share = chan_width // groups
    seq_length = seq_count * local_length
    factor = (batch_count * seq_length) ** (-0.5)
    mixed = (key_rows * value_rows).astype(jnp.bfloat16)
    weighted = (cot_rows * query_rows).astype(jnp.bfloat16)

    mixed_wide = mixed.astype(jnp.float32)
    weighted_wide = weighted.astype(jnp.float32)
    gain_part = jnp.sum(weighted_wide * mixed_wide, axis=0)

    pair = jnp.stack([mixed.T, weighted.T], axis=0).reshape(2, groups, share, local_length)
    pair = jnp.transpose(pair, (1, 0, 2, 3)).reshape(groups, 2 * share, local_length)
    half_length = local_length // batch_count
    taps_t = long_filter.T.reshape(groups, share, batch_count, half_length)
    taps_mine = lax.dynamic_index_in_dim(taps_t, lax.axis_index("dp"), axis=2, keepdims=False)
    taps_rows = share * half_length // local_length
    taps_mine = taps_mine.astype(jnp.bfloat16).reshape(groups, taps_rows, local_length)
    taps_got = lax.all_to_all(taps_mine, ("seq", "dp"), 0, 0, tiled=True)
    taps_got, pair = lax.optimization_barrier((taps_got, pair))
    got = lax.all_to_all(pair, ("seq", "dp"), 0, 0, tiled=True)
    taps_t = taps_got.reshape(seq_count, batch_count, share, half_length)
    taps = jnp.transpose(taps_t, (0, 1, 3, 2)).reshape(seq_length, 1, share)
    taps = jnp.broadcast_to(taps, (seq_length, 2 * batch_count, share)).reshape(
        seq_length, 2 * batch_count * share
    )
    tables, taps_first = taps_spectrum_first(taps.astype(jnp.float32))
    gain_part, got, tables, taps_first = lax.optimization_barrier(
        (gain_part, got, tables, taps_first)
    )
    total = gain_part
    distance = 1
    while distance < groups:
        partners = [(i, i ^ distance) for i in range(groups)]
        total = total + lax.ppermute(total, ("seq", "dp"), partners)
        distance *= 2
    grad_skip = factor * total

    pair_t = got.reshape(seq_count, batch_count, 2, share, local_length)
    signals = jnp.transpose(pair_t, (0, 4, 2, 1, 3)).reshape(seq_length, 2 * batch_count * share)

    tables, pair_spec, cross_spec, grad_skip = spectral_products(
        signals.astype(jnp.float32), taps_first, tables, grad_skip
    )
    pair_vals = spectral_inverse(pair_spec, tables)
    pair_vals = pair_vals.reshape(seq_length, 2, batch_count, share)

    pair_back = pair_vals.astype(jnp.bfloat16).reshape(
        seq_count, local_length, 2, batch_count, share
    )
    pair_back = jnp.transpose(pair_back, (0, 3, 2, 4, 1)).reshape(
        groups, 2 * share, local_length
    )
    pair_home = lax.all_to_all(pair_back, ("seq", "dp"), 0, 0, tiled=True)

    cross = spectral_inverse(cross_spec, tables)
    cross = cross.reshape(seq_length, 2, batch_count, share)
    slope = jnp.sum(cross[:, 0], axis=1)
    slope_blocks = jnp.swapaxes(slope.astype(jnp.bfloat16).reshape(seq_count, local_length, share), 1, 2)
    slope_send = jnp.broadcast_to(
        slope_blocks[:, None], (seq_count, batch_count, share, local_length)
    ).reshape(groups, share, local_length)
    pair_home, slope_send = lax.optimization_barrier((pair_home, slope_send))
    slope_home = lax.all_to_all(slope_send, ("seq", "dp"), 0, 0, tiled=True)

    pair_home = pair_home.reshape(groups, 2, share, local_length)
    pair_home = jnp.transpose(pair_home, (1, 0, 2, 3)).reshape(2, chan_width, local_length)
    conv_rows = pair_home[0].T.astype(jnp.float32)
    corr_rows = pair_home[1].T.astype(jnp.float32)
    grad_filter = factor * slope_home.reshape(chan_width, local_length).T.astype(jnp.float32)

    signal = conv_rows + skip_gain[None, :] * mixed_wide
    output = (query_rows * signal).astype(jnp.bfloat16)
    grad_query = (cot_rows * signal).astype(jnp.bfloat16)
    back = corr_rows + skip_gain[None, :] * weighted_wide
    grad_key = (back * value_rows).astype(jnp.bfloat16)
    grad_value = (back * key_rows).astype(jnp.bfloat16)
    return (
        output[None],
        grad_query[None],
        grad_key[None],
        grad_value[None],
        grad_filter,
        grad_skip,
    )


def solution(mesh):
    return jax.shard_map(
        on_device,
        mesh=mesh,
        in_specs=(
            P("dp", "seq", "chan"),
            P("dp", "seq", "chan"),
            P("dp", "seq", "chan"),
            P("dp", "seq", "chan"),
            P("seq", "chan"),
            P("chan"),
        ),
        out_specs=(
            P("dp", "seq", "chan"),
            P("dp", "seq", "chan"),
            P("dp", "seq", "chan"),
            P("dp", "seq", "chan"),
            P("seq", "chan"),
            P("chan"),
        ),
        check_vma=False,
    )
```
